256 devices in a mesh: ctx: 32 (over z, x_lo, core), heads: 8 (over x_hi, y).
Axes of the slice: x: 4 (x_hi: 2, x_lo: 2; x = x_hi * 2 + x_lo), y: 4, z: 8, core: 2. Of those that a mesh axis runs over, the one named last changes fastest.
Arguments:
- hidden: bfloat16 [16384, 5376], P(('ctx', 'heads')), may hold values from -8 to 8
- query_weight: bfloat16 [5376, 2048], P(None, 'heads'), may hold values from -0.5 to 0.5
- key_weight: bfloat16 [5376, 1024], P(None, 'heads'), may hold values from -0.5 to 0.5
- value_weight: bfloat16 [5376, 1024], P(None, 'heads'), may hold values from -0.078125 to 0.078125
- query_gain: float32 [128], replicated, may hold values from 0.5 to 6
- key_gain: float32 [128], replicated, may hold values from 0.5 to 6
- out_grad: bfloat16 [16384, 2048], P('ctx', 'heads'), may hold values from -6 to 6
Outputs:
- attention: bfloat16 [16384, 2048], P('ctx', 'heads')
- input_grad: bfloat16 [16384, 5376], P(('ctx', 'heads'))
- query_weight_grad: float32 [5376, 2048], P('ctx', 'heads')
- key_weight_grad: float32 [5376, 1024], P('ctx', 'heads')
- value_weight_grad: float32 [5376, 1024], P('ctx', 'heads')
The draws below stay inside these ranges and needn't reach their ends.
All inputs are finite; a program needn't handle non-finite values.
Results may differ from the reference program's by a relative error of at most 0.039.
Values may be sent and summed in bfloat16 or wider, within the bound.
No kernel may reach another device: no remote copies, remote signals or barrier semaphores. Data moves between devices by JAX's collectives and lax.ppermute only.
A program may use at most 128 MiB of HBM per device.

```python
import math
import jax
import jax.numpy as jnp
from jax import lax

D = 5376
HEAD_DIM = 128
WINDOW = 1024
SCALAR = 168
HEADS = 16
KV_HEADS = 8
TOK_DEV = 512
TOKENS = 16384
HEAD_GROUPS = 8


def key_columns(key):
    return jax.random.normal(jax.random.fold_in(key, 7), (D, KV_HEADS * HEAD_DIM), jnp.float32) * D ** (-0.5)


def draw_key_weight(key, part):
    return jnp.clip(key_columns(key), -0.5, 0.5).astype(jnp.bfloat16)


def draw_query_weight(key, part):
    independent = jax.random.normal(jax.random.fold_in(key, 11), (D, HEADS * HEAD_DIM), jnp.float32) * D ** (-0.5)
    return jnp.clip(independent, -0.5, 0.5).astype(jnp.bfloat16)


def draw_hidden(key, part):
    values = jax.random.normal(jax.random.fold_in(key, 29), (TOKENS, D), jnp.float32)
    return jnp.clip(values, -8.0, 8.0).astype(jnp.bfloat16)


def channel_gains(key, salt_value):
    return jax.random.uniform(jax.random.fold_in(key, salt_value), (HEAD_DIM,), jnp.float32, 0.5, 1.5)


def draw_query_gain(key, part):
    return channel_gains(key, 41)


def draw_key_gain(key, part):
    return channel_gains(key, 43)


def block_levels(stream_key, shape, cuts, low, high):
    def one(position, parts):
        draws = jax.random.uniform(jax.random.fold_in(jax.random.fold_in(stream_key, 6), position), (parts,), jnp.float32, low / len(cuts), high / len(cuts))
        return jnp.repeat(jnp.exp(draws), shape[position] // parts).reshape((-1,) + (1,) * (len(shape) - position - 1))

    loudness = one(*cuts[0])
    for cut in cuts[1:]:
        loudness = loudness * one(*cut)
    return loudness


def bell_draw(rng, extent, scale, bound, split=(), held_as=jnp.bfloat16):
    drawn = scale * jax.random.normal(rng, extent, jnp.float32)
    if split:
        drawn = drawn * block_levels(rng, extent, split, -0.22, 0.18)
    return jnp.clip(drawn, -bound, bound).astype(held_as)


def setup_inputs(seed: int = 0) -> dict:
    arg_keys = jax.random.split(jax.random.key(seed), 8)
    hidden = draw_hidden(jax.random.fold_in(arg_keys[7], 71), 0)
    query_weight = draw_query_weight(jax.random.fold_in(arg_keys[7], 71), 0)
    key_weight = draw_key_weight(jax.random.fold_in(arg_keys[7], 71), 0)
    value_weight = bell_draw(arg_keys[3], (D, KV_HEADS * HEAD_DIM), D ** -0.5, 0.078125, ((1, 8),))
    query_gain = draw_query_gain(jax.random.fold_in(arg_keys[7], 71), 0)
    key_gain = draw_key_gain(jax.random.fold_in(arg_keys[7], 71), 0)
    out_grad = bell_draw(arg_keys[6], (TOKENS, HEADS * HEAD_DIM), 1.0, 6.0, ((0, 32), (1, 8)))
    return {"hidden": hidden, "query_weight": query_weight, "key_weight": key_weight, "value_weight": value_weight, "query_gain": query_gain, "key_gain": key_gain, "out_grad": out_grad}


def rope_tables(positions, head_size):
    half_size = head_size // 2
    indices = jnp.arange(half_size, dtype=jnp.float32)
    inverse = jnp.exp(indices * (-2.0 * math.log(10000.0) / head_size))
    angles = positions.astype(jnp.float32)[:, None] * inverse[None, :]
    return (jnp.cos(angles), jnp.sin(angles))

def prepare(projected, cosine, sine_table, channel_gain, factor):
    row_count = projected.shape[0]
    head_size = channel_gain.shape[0]
    pieces = projected.reshape(row_count, -1, head_size)
    normed = pieces * lax.rsqrt(lax.optimization_barrier(jnp.mean(pieces * pieces, axis=-1, keepdims=True)) + 1e-06) * channel_gain
    half_size = head_size // 2
    leading = normed[..., :half_size]
    trailing = normed[..., half_size:]
    cos_rows = cosine[:, None, :]
    sin_rows = sine_table[:, None, :]
    turned = jnp.concatenate([leading * cos_rows - trailing * sin_rows, trailing * cos_rows + leading * sin_rows], axis=-1)
    return (turned * factor).reshape(row_count, -1)

def band_mask(query_pos, key_pos):
    separation = query_pos[:, None] - key_pos[None, :]
    return (separation >= 0) & (separation < WINDOW) & (key_pos[None, :] >= 0)

def head_grids(query_block, key_window, value_window, group_size):
    query_grid = query_block.reshape(query_block.shape[0], -1, group_size, HEAD_DIM).astype(jnp.float32)
    key_grid = key_window.reshape(key_window.shape[0], -1, HEAD_DIM).astype(jnp.float32)
    value_grid = value_window.reshape(value_window.shape[0], -1, HEAD_DIM).astype(jnp.float32)
    return (query_grid, key_grid, value_grid)

def attend_forward(query_block, key_window, value_window, allowed, group_size):
    query_grid, key_grid, value_grid = head_grids(query_block, key_window, value_window, group_size)
    scores = jnp.einsum('qkgd,jkd->kgqj', query_grid, key_grid)
    masked = jnp.where(allowed, scores, -1e+30)
    highest = lax.optimization_barrier(jnp.max(masked, axis=-1, keepdims=True))
    total = lax.optimization_barrier(jnp.sum(jnp.exp(masked - highest), axis=-1, keepdims=True))
    log_total = highest + jnp.log(total)
    weights = jnp.where(allowed, jnp.exp(masked - log_total), 0.0)
    weights_low = lax.optimization_barrier(weights.astype(jnp.bfloat16)).astype(jnp.float32)
    output = jnp.einsum('kgqj,jkd->qkgd', weights_low, value_grid)
    return (output.reshape(query_block.shape[0], -1), log_total[..., 0])

def attend_backward(query_block, key_window, value_window, allowed, log_total, out_block, attention_block, group_size):
    query_grid, key_grid, value_grid = head_grids(query_block, key_window, value_window, group_size)
    row_count = query_block.shape[0]
    grad_grid = out_block.reshape(row_count, -1, group_size, HEAD_DIM).astype(jnp.float32)
    attention_grid = attention_block.reshape(row_count, -1, group_size, HEAD_DIM).astype(jnp.float32)
    scores = jnp.einsum('qkgd,jkd->kgqj', query_grid, key_grid)
    masked = jnp.where(allowed, scores, -1e+30)
    weights = jnp.where(allowed, jnp.exp(masked - log_total[..., None]), 0.0)
    weights_low = lax.optimization_barrier(weights.astype(jnp.bfloat16)).astype(jnp.float32)
    delta = jnp.einsum('qkgd,qkgd->kgq', grad_grid, attention_grid)
    products = jnp.einsum('qkgd,jkd->kgqj', grad_grid, value_grid)
    shifts = (weights * (products - delta[..., None])).astype(jnp.bfloat16)
    shifts = lax.optimization_barrier(shifts).astype(jnp.float32)
    query_cot = jnp.einsum('kgqj,jkd->qkgd', shifts, key_grid).reshape(row_count, -1)
    key_cot = jnp.einsum('kgqj,qkgd->jkd', shifts, query_grid).reshape(key_window.shape[0], -1)
    value_cot = jnp.einsum('kgqj,qkgd->jkd', weights_low, grad_grid).reshape(key_window.shape[0], -1)
    return (query_cot, key_cot, value_cot)

def reference(hidden, query_weight, key_weight, value_weight, query_gain, key_gain, out_grad):
    group_size = HEADS // KV_HEADS
    block_rows = min(TOK_DEV, 512)
    block_count = TOKENS // block_rows
    window_rows = block_rows + WINDOW
    positions = jnp.arange(TOKENS, dtype=jnp.int32)
    cosine, sine_table = rope_tables(positions, HEAD_DIM)
    query_proj = jnp.dot(hidden, query_weight, preferred_element_type=jnp.float32)
    key_proj = jnp.dot(hidden, key_weight, preferred_element_type=jnp.float32)
    value_proj = jnp.dot(hidden, value_weight, preferred_element_type=jnp.float32)
    query_full, query_back = jax.vjp(lambda projected: prepare(projected, cosine, sine_table, query_gain, SCALAR ** (-0.5)), query_proj)
    key_full, key_back = jax.vjp(lambda projected: prepare(projected, cosine, sine_table, key_gain, 1.0), key_proj)
    query_cast = lax.optimization_barrier(query_full.astype(jnp.bfloat16))
    key_cast = lax.optimization_barrier(key_full.astype(jnp.bfloat16))
    value_cast = lax.optimization_barrier(value_proj.astype(jnp.bfloat16))
    key_padded = jnp.pad(key_cast, ((WINDOW, 0), (0, 0)))
    value_padded = jnp.pad(value_cast, ((WINDOW, 0), (0, 0)))

    def window_of(block_index):
        block_start = block_index * block_rows
        query_block = lax.dynamic_slice_in_dim(query_cast, block_start, block_rows, 0)
        key_window = lax.dynamic_slice_in_dim(key_padded, block_start, window_rows, 0)
        value_window = lax.dynamic_slice_in_dim(value_padded, block_start, window_rows, 0)
        query_pos = block_start + jnp.arange(block_rows, dtype=jnp.int32)
        key_pos = block_start - WINDOW + jnp.arange(window_rows, dtype=jnp.int32)
        return (query_block, key_window, value_window, band_mask(query_pos, key_pos))

    def forward_block(block_index):
        query_block, key_window, value_window, allowed = window_of(block_index)
        return attend_forward(query_block, key_window, value_window, allowed, group_size)
    outputs, log_totals = lax.map(forward_block, jnp.arange(block_count, dtype=jnp.int32))
    attention = outputs.reshape(TOKENS, -1).astype(jnp.bfloat16)

    def backward_block(carry, block_index):
        key_acc, value_acc = carry
        query_block, key_window, value_window, allowed = window_of(block_index)
        block_start = block_index * block_rows
        out_block = lax.dynamic_slice_in_dim(out_grad, block_start, block_rows, 0)
        attention_block = lax.dynamic_slice_in_dim(attention, block_start, block_rows, 0)
        query_cot, key_cot, value_cot = attend_backward(query_block, key_window, value_window, allowed, log_totals[block_index], out_block, attention_block, group_size)
        key_region = lax.dynamic_slice_in_dim(key_acc, block_start, window_rows, 0) + key_cot
        value_region = lax.dynamic_slice_in_dim(value_acc, block_start, window_rows, 0) + value_cot
        key_acc = lax.dynamic_update_slice_in_dim(key_acc, key_region, block_start, 0)
        value_acc = lax.dynamic_update_slice_in_dim(value_acc, value_region, block_start, 0)
        return ((key_acc, value_acc), query_cot)
    zero_rows = jnp.zeros((TOKENS + WINDOW, KV_HEADS * HEAD_DIM), jnp.float32)
    (key_acc, value_acc), query_cots = lax.scan(backward_block, (zero_rows, zero_rows), jnp.arange(block_count, dtype=jnp.int32))
    grad_query = query_back(query_cots.reshape(TOKENS, -1))[0].astype(jnp.bfloat16)
    grad_key = key_back(key_acc[WINDOW:])[0].astype(jnp.bfloat16)
    grad_value = value_acc[WINDOW:].astype(jnp.bfloat16)
    grad_scale = float(TOKENS) ** (-0.5)
    contract = (((0,), (0,)), ((), ()))
    query_weight_grad = lax.dot_general(hidden, grad_query, contract, preferred_element_type=jnp.float32) * grad_scale
    key_weight_grad = lax.dot_general(hidden, grad_key, contract, preferred_element_type=jnp.float32) * grad_scale
    value_weight_grad = lax.dot_general(hidden, grad_value, contract, preferred_element_type=jnp.float32) * grad_scale
    query_width = HEADS * HEAD_DIM // HEAD_GROUPS
    key_width = KV_HEADS * HEAD_DIM // HEAD_GROUPS
    back_contract = (((1,), (1,)), ((), ()))
    input_sum = jnp.zeros((TOKENS, D), jnp.float32)
    for group_index in range(HEAD_GROUPS):
        query_lower = group_index * query_width
        key_lower = group_index * key_width
        group_term = lax.dot_general(grad_query[:, query_lower:query_lower + query_width], query_weight[:, query_lower:query_lower + query_width], back_contract, preferred_element_type=jnp.float32)
        group_term = group_term + lax.dot_general(grad_key[:, key_lower:key_lower + key_width], key_weight[:, key_lower:key_lower + key_width], back_contract, preferred_element_type=jnp.float32)
        group_term = group_term + lax.dot_general(grad_value[:, key_lower:key_lower + key_width], value_weight[:, key_lower:key_lower + key_width], back_contract, preferred_element_type=jnp.float32)
        input_sum = input_sum + lax.optimization_barrier(group_term.astype(jnp.bfloat16)).astype(jnp.float32)
    return (attention, input_sum.astype(jnp.bfloat16), query_weight_grad, key_weight_grad, value_weight_grad)
```

```python
import math

import jax
import jax.numpy as jnp
from jax import lax
from jax.sharding import PartitionSpec as P

HEAD_DIM = 128
WINDOW = 1024
SCALAR = 168
HEADS = 16
KV_HEADS = 8


def passed_along(block, axis, distance):
    devices = range(lax.axis_size(axis))
    route = [(i - distance, i) for i in devices if i - distance in devices]
    return lax.ppermute(block, axis, route)


def torus_shifts(axis):
    size = lax.axis_size(axis)
    inner = size // 2 if size >= 4 else size
    outer = size // inner
    me = lax.axis_index(axis)

    def moved(index, dx, dy):
        return ((index // inner + dx) % outer) * inner + (index % inner + dy) % inner

    shifts = [(dx, dy) for dx in range(outer) for dy in range(inner)][1:]
    routes = [[(i, moved(i, dx, dy)) for i in range(size)] for dx, dy in shifts]
    targets = [moved(me, dx, dy) for dx, dy in shifts]
    slot_of = [
        ((me // inner - j // inner) % outer) * inner + (me % inner - j % inner) % inner
        for j in range(size)
    ]
    return (size, me, routes, targets, slot_of)


def gather_over(block, axis):
    size, me, routes, targets, slot_of = torus_shifts(axis)
    slots = jnp.stack([block] + [lax.ppermute(block, axis, route) for route in routes])
    order = jnp.stack([jnp.asarray(s, jnp.int32) for s in slot_of])
    return jnp.take(slots, order, axis=0).reshape((size * block.shape[0],) + block.shape[1:])


def scatter_sum_over(full, axis):
    size, me, routes, targets, slot_of = torus_shifts(axis)
    pieces = full.reshape((size, full.shape[0] // size) + full.shape[1:])
    total = lax.dynamic_index_in_dim(pieces, me, 0, keepdims=False).astype(jnp.float32)
    for route, target in zip(routes, targets):
        piece = lax.dynamic_index_in_dim(pieces, target, 0, keepdims=False)
        total = total + lax.ppermute(piece, axis, route).astype(jnp.float32)
    return total


def rope_tables(positions, head_size):
    half_size = head_size // 2
    indices = jnp.arange(half_size, dtype=jnp.float32)
    inverse = jnp.exp(indices * (-2.0 * math.log(10000.0) / head_size))
    angles = positions.astype(jnp.float32)[:, None] * inverse[None, :]
    return (jnp.cos(angles), jnp.sin(angles))


def prepare(projected, cosine, sine_table, channel_gain, factor):
    row_count = projected.shape[0]
    head_size = channel_gain.shape[0]
    pieces = projected.reshape(row_count, -1, head_size)
    normed = (
        pieces * lax.rsqrt(jnp.mean(pieces * pieces, axis=-1, keepdims=True) + 1e-06) * channel_gain
    )
    half_size = head_size // 2
    leading = normed[..., :half_size]
    trailing = normed[..., half_size:]
    cos_rows = cosine[:, None, :]
    sin_rows = sine_table[:, None, :]
    turned = jnp.concatenate(
        [leading * cos_rows - trailing * sin_rows, trailing * cos_rows + leading * sin_rows],
        axis=-1,
    )
    return (turned * factor).reshape(row_count, -1)


def band_mask(query_pos, key_pos):
    separation = query_pos[:, None] - key_pos[None, :]
    return (separation >= 0) & (separation < WINDOW) & (key_pos[None, :] >= 0)


def head_grids(query_block, key_window, value_window, group_size):
    query_grid = query_block.reshape(query_block.shape[0], -1, group_size, HEAD_DIM)
    key_grid = key_window.reshape(key_window.shape[0], -1, HEAD_DIM)
    value_grid = value_window.reshape(value_window.shape[0], -1, HEAD_DIM)
    return (query_grid, key_grid, value_grid)


def attend_forward(query_block, key_window, value_window, allowed, group_size):
    query_grid, key_grid, value_grid = head_grids(query_block, key_window, value_window, group_size)
    scores = jnp.einsum("qkgd,jkd->kgqj", query_grid, key_grid, preferred_element_type=jnp.float32)
    masked = jnp.where(allowed, scores, -1e30)
    highest = jnp.max(masked, axis=-1, keepdims=True)
    total = jnp.sum(jnp.exp(masked - highest), axis=-1, keepdims=True)
    log_total = highest + jnp.log(total)
    weights = jnp.where(allowed, jnp.exp(masked - log_total), 0.0)
    output = jnp.einsum(
        "kgqj,jkd->qkgd",
        weights.astype(jnp.bfloat16),
        value_grid,
        preferred_element_type=jnp.float32,
    )
    return (output.reshape(query_block.shape[0], -1), log_total[..., 0])


def attend_backward(
    query_block,
    key_window,
    value_window,
    allowed,
    log_total,
    out_block,
    attention_block,
    group_size,
):
    query_grid, key_grid, value_grid = head_grids(query_block, key_window, value_window, group_size)
    row_count = query_block.shape[0]
    grad_grid = out_block.reshape(row_count, -1, group_size, HEAD_DIM)
    attention_grid = attention_block.reshape(row_count, -1, group_size, HEAD_DIM)
    scores = jnp.einsum("qkgd,jkd->kgqj", query_grid, key_grid, preferred_element_type=jnp.float32)
    masked = jnp.where(allowed, scores, -1e30)
    weights = jnp.where(allowed, jnp.exp(masked - log_total[..., None]), 0.0)
    delta = jnp.einsum(
        "qkgd,qkgd->kgq", grad_grid, attention_grid, preferred_element_type=jnp.float32
    )
    products = jnp.einsum(
        "qkgd,jkd->kgqj", grad_grid, value_grid, preferred_element_type=jnp.float32
    )
    shifts = (weights * (products - delta[..., None])).astype(jnp.bfloat16)
    query_cot = jnp.einsum(
        "kgqj,jkd->qkgd", shifts, key_grid, preferred_element_type=jnp.float32
    ).reshape(row_count, -1)
    key_cot = jnp.einsum(
        "kgqj,qkgd->jkd", shifts, query_grid, preferred_element_type=jnp.float32
    ).reshape(key_window.shape[0], -1)
    value_cot = jnp.einsum(
        "kgqj,qkgd->jkd",
        weights.astype(jnp.bfloat16),
        grad_grid,
        preferred_element_type=jnp.float32,
    ).reshape(key_window.shape[0], -1)
    return (query_cot, key_cot, value_cot)


def per_device(hidden, query_weight, key_weight, value_weight, query_gain, key_gain, out_grad):
    token_count = out_grad.shape[0]
    group_size = HEADS // KV_HEADS
    block_rows = min(token_count, 512)
    block_count = token_count // block_rows
    window_rows = block_rows + WINDOW
    reach_blocks = (WINDOW - 2) // token_count + 1
    position_base = lax.axis_index("ctx") * token_count
    gathered = gather_over(hidden, "heads")
    query_proj = jnp.dot(gathered, query_weight, preferred_element_type=jnp.float32)
    key_proj = jnp.dot(gathered, key_weight, preferred_element_type=jnp.float32)
    value_proj = jnp.dot(gathered, value_weight, preferred_element_type=jnp.float32)
    positions = position_base + jnp.arange(token_count, dtype=jnp.int32)
    cosine, sine_table = rope_tables(positions, HEAD_DIM)
    query_full, query_back = jax.vjp(
        lambda projected: prepare(projected, cosine, sine_table, query_gain, SCALAR ** (-0.5)),
        query_proj,
    )
    key_full, key_back = jax.vjp(
        lambda projected: prepare(projected, cosine, sine_table, key_gain, 1.0), key_proj
    )
    query_cast = query_full.astype(jnp.bfloat16)
    key_value = jnp.stack([key_full.astype(jnp.bfloat16), value_proj.astype(jnp.bfloat16)])
    received = [passed_along(key_value, "ctx", distance) for distance in range(1, reach_blocks + 1)]
    window_pair = jnp.concatenate(received[::-1] + [key_value], axis=1)
    key_span = window_pair[0]
    value_span = window_pair[1]

    def window_of(block_index):
        block_start = block_index * block_rows
        query_pos = position_base + block_start + jnp.arange(block_rows, dtype=jnp.int32)
        key_pos = position_base - WINDOW + block_start + jnp.arange(window_rows, dtype=jnp.int32)
        return (query_cast, key_span, value_span, band_mask(query_pos, key_pos))

    def forward_block(block_index):
        query_block, key_window, value_window, allowed = window_of(block_index)
        return attend_forward(query_block, key_window, value_window, allowed, group_size)

    outputs, log_totals = lax.map(forward_block, jnp.arange(block_count, dtype=jnp.int32))
    attention = outputs.reshape(token_count, -1).astype(jnp.bfloat16)

    def backward_block(block_index, carry):
        query_acc, pair_acc = carry
        query_block, key_window, value_window, allowed = window_of(block_index)
        block_start = block_index * block_rows
        query_cot, key_cot, value_cot = attend_backward(
            query_block,
            key_window,
            value_window,
            allowed,
            log_totals[block_index],
            out_grad,
            attention,
            group_size,
        )
        query_acc = query_cot
        region = pair_acc + jnp.stack([key_cot, value_cot])
        pair_acc = region
        return (query_acc, pair_acc)

    query_zero = jnp.zeros((token_count, query_weight.shape[1]), jnp.float32)
    pair_zero = jnp.zeros((2, (reach_blocks + 1) * token_count, key_weight.shape[1]), jnp.float32)
    query_acc, pair_acc = lax.fori_loop(0, block_count, backward_block, (query_zero, pair_zero))
    grad_query = query_back(query_acc)[0].astype(jnp.bfloat16)
    grad_scale = float(lax.axis_size("ctx") * token_count) ** (-0.5)
    contract = (((0,), (0,)), ((), ()))
    own_pair = pair_acc[:, reach_blocks * token_count :]
    for distance in range(1, reach_blocks + 1):
        lower_row = (reach_blocks - distance) * token_count
        own_pair = own_pair + passed_along(
            pair_acc[:, lower_row : lower_row + token_count], "ctx", -distance
        )
    grad_key = key_back(own_pair[0])[0].astype(jnp.bfloat16)
    grad_value = own_pair[1].astype(jnp.bfloat16)
    key_width = key_weight.shape[1]
    query_width = query_weight.shape[1]
    summed = lax.psum_scatter(
        (
            lax.dot_general(
                gathered,
                jnp.concatenate([grad_query, grad_key, grad_value], axis=1),
                contract,
                preferred_element_type=jnp.float32,
            )
            * grad_scale
        ).astype(jnp.bfloat16),
        "ctx",
        scatter_dimension=0,
        tiled=True,
    ).astype(jnp.float32)
    query_weight_grad = summed[:, :query_width]
    key_weight_grad = summed[:, query_width : query_width + key_width]
    value_weight_grad = summed[:, query_width + key_width :]
    back_contract = (((1,), (1,)), ((), ()))
    partial_sum = lax.dot_general(
        grad_query, query_weight, back_contract, preferred_element_type=jnp.float32
    )
    partial_sum = partial_sum + lax.dot_general(
        grad_key, key_weight, back_contract, preferred_element_type=jnp.float32
    )
    input_grad = scatter_sum_over(
        (
            partial_sum
            + lax.dot_general(
                grad_value, value_weight, back_contract, preferred_element_type=jnp.float32
            )
        ).astype(jnp.bfloat16),
        "heads",
    ).astype(jnp.bfloat16)
    return (attention, input_grad, query_weight_grad, key_weight_grad, value_weight_grad)


def solution(mesh):
    return jax.shard_map(
        per_device,
        mesh=mesh,
        in_specs=(
            P(("ctx", "heads"), None),
            P(None, "heads"),
            P(None, "heads"),
            P(None, "heads"),
            P(),
            P(),
            P("ctx", "heads"),
        ),
        out_specs=(
            P("ctx", "heads"),
            P(("ctx", "heads"), None),
            P("ctx", "heads"),
            P("ctx", "heads"),
            P("ctx", "heads"),
        ),
        check_vma=False,
    )
```

```python
import math

import jax
import jax.numpy as jnp
from jax import lax
from jax.sharding import PartitionSpec as P

HEAD_DIM = 128
WINDOW = 1024
SCALAR = 168
HEADS = 16
KV_HEADS = 8


def passed_along(block, axis, distance):
    devices = range(lax.axis_size(axis))
    route = [(i - distance, i) for i in devices if i - distance in devices]
    return lax.ppermute(block, axis, route)


def torus_shifts(axis):
    size = lax.axis_size(axis)
    inner = size // 2 if size >= 4 else size
    outer = size // inner
    me = lax.axis_index(axis)

    def moved(index, dx, dy):
        return ((index // inner + dx) % outer) * inner + (index % inner + dy) % inner

    shifts = [(dx, dy) for dx in range(outer) for dy in range(inner)][1:]
    routes = [[(i, moved(i, dx, dy)) for i in range(size)] for dx, dy in shifts]
    targets = [moved(me, dx, dy) for dx, dy in shifts]
    slot_of = [
        ((me // inner - j // inner) % outer) * inner + (me % inner - j % inner) % inner
        for j in range(size)
    ]
    return (size, me, routes, targets, slot_of)


def gather_over(block, axis):
    size, me, routes, targets, slot_of = torus_shifts(axis)
    slots = jnp.stack([block] + [lax.ppermute(block, axis, route) for route in routes])
    order = jnp.stack([jnp.asarray(s, jnp.int32) for s in slot_of])
    return jnp.take(slots, order, axis=0).reshape((size * block.shape[0],) + block.shape[1:])


def scatter_sum_over(full, axis):
    size, me, routes, targets, slot_of = torus_shifts(axis)
    pieces = full.reshape((size, full.shape[0] // size) + full.shape[1:])
    total = lax.dynamic_index_in_dim(pieces, me, 0, keepdims=False).astype(jnp.float32)
    for route, target in zip(routes, targets):
        piece = lax.dynamic_index_in_dim(pieces, target, 0, keepdims=False)
        total = total + lax.ppermute(piece, axis, route).astype(jnp.float32)
    return total


def ring_scatter_sum(blocks, axis, count, stride, forward):
    size = lax.axis_size(axis)
    me = lax.axis_index(axis)
    digit = (me // stride) % count
    step = 1 if forward else -1
    route = [
        (i, i - ((i // stride) % count) * stride + (((i // stride) % count + step) % count) * stride)
        for i in range(size)
    ]

    def chunk(k):
        return lax.dynamic_index_in_dim(blocks, (digit - step * (k + 1)) % count, 0, keepdims=False)

    running = chunk(0)
    for k in range(count - 1):
        running = lax.ppermute(running.astype(jnp.bfloat16), axis, route).astype(jnp.float32) + chunk(k + 1)
    return running


def pair_scatter_sum(blocks, axis, stride):
    size = lax.axis_size(axis)
    me = lax.axis_index(axis)
    digit = (me // stride) % 2
    route = [(i, i + stride if (i // stride) % 2 == 0 else i - stride) for i in range(size)]
    own = lax.dynamic_index_in_dim(blocks, digit, 0, keepdims=False)
    other = lax.dynamic_index_in_dim(blocks, 1 - digit, 0, keepdims=False)
    return own + lax.ppermute(other.astype(jnp.bfloat16), axis, route).astype(jnp.float32)


def ctx_scatter_sum(full, axis, levels):
    outer, middle, inner = levels
    width = full.shape[1]
    grid = full.reshape(outer, middle, inner, -1, width)
    grid = jnp.moveaxis(grid, 2, 0)
    grid = pair_scatter_sum(grid, axis, 1)
    half = width // 2
    up = ring_scatter_sum(grid[..., :half], axis, outer, middle * inner, True)
    down = ring_scatter_sum(grid[..., half:], axis, outer, middle * inner, False)
    grid = jnp.concatenate([up, down], axis=-1)
    return pair_scatter_sum(grid, axis, inner)


def rope_tables(positions, head_size):
    half_size = head_size // 2
    indices = jnp.arange(half_size, dtype=jnp.float32)
    inverse = jnp.exp(indices * (-2.0 * math.log(10000.0) / head_size))
    angles = positions.astype(jnp.float32)[:, None] * inverse[None, :]
    return (jnp.cos(angles), jnp.sin(angles))


def prepare(projected, cosine, sine_table, channel_gain, factor):
    row_count = projected.shape[0]
    head_size = channel_gain.shape[0]
    pieces = projected.reshape(row_count, -1, head_size)
    normed = (
        pieces * lax.rsqrt(jnp.mean(pieces * pieces, axis=-1, keepdims=True) + 1e-06) * channel_gain
    )
    half_size = head_size // 2
    leading = normed[..., :half_size]
    trailing = normed[..., half_size:]
    cos_rows = cosine[:, None, :]
    sin_rows = sine_table[:, None, :]
    turned = jnp.concatenate(
        [leading * cos_rows - trailing * sin_rows, trailing * cos_rows + leading * sin_rows],
        axis=-1,
    )
    return (turned * factor).reshape(row_count, -1)


def band_mask(query_pos, key_pos):
    separation = query_pos[:, None] - key_pos[None, :]
    return (separation >= 0) & (separation < WINDOW) & (key_pos[None, :] >= 0)


def head_grids(query_block, key_window, value_window, group_size):
    query_grid = query_block.reshape(query_block.shape[0], -1, group_size, HEAD_DIM)
    key_grid = key_window.reshape(key_window.shape[0], -1, HEAD_DIM)
    value_grid = value_window.reshape(value_window.shape[0], -1, HEAD_DIM)
    return (query_grid, key_grid, value_grid)


def attend_forward(query_block, key_window, value_window, allowed, group_size):
    query_grid, key_grid, value_grid = head_grids(query_block, key_window, value_window, group_size)
    scores = jnp.einsum("qkgd,jkd->kgqj", query_grid, key_grid, preferred_element_type=jnp.float32)
    masked = jnp.where(allowed, scores, -1e30)
    highest = jnp.max(masked, axis=-1, keepdims=True)
    total = jnp.sum(jnp.exp(masked - highest), axis=-1, keepdims=True)
    log_total = highest + jnp.log(total)
    weights = jnp.where(allowed, jnp.exp(masked - log_total), 0.0)
    output = jnp.einsum(
        "kgqj,jkd->qkgd",
        weights.astype(jnp.bfloat16),
        value_grid,
        preferred_element_type=jnp.float32,
    )
    return (output.reshape(query_block.shape[0], -1), log_total[..., 0])


def attend_backward(
    query_block,
    key_window,
    value_window,
    allowed,
    log_total,
    out_block,
    attention_block,
    group_size,
):
    query_grid, key_grid, value_grid = head_grids(query_block, key_window, value_window, group_size)
    row_count = query_block.shape[0]
    grad_grid = out_block.reshape(row_count, -1, group_size, HEAD_DIM)
    attention_grid = attention_block.reshape(row_count, -1, group_size, HEAD_DIM)
    scores = jnp.einsum("qkgd,jkd->kgqj", query_grid, key_grid, preferred_element_type=jnp.float32)
    masked = jnp.where(allowed, scores, -1e30)
    weights = jnp.where(allowed, jnp.exp(masked - log_total[..., None]), 0.0)
    delta = jnp.einsum(
        "qkgd,qkgd->kgq", grad_grid, attention_grid, preferred_element_type=jnp.float32
    )
    products = jnp.einsum(
        "qkgd,jkd->kgqj", grad_grid, value_grid, preferred_element_type=jnp.float32
    )
    shifts = (weights * (products - delta[..., None])).astype(jnp.bfloat16)
    query_cot = jnp.einsum(
        "kgqj,jkd->qkgd", shifts, key_grid, preferred_element_type=jnp.float32
    ).reshape(row_count, -1)
    key_cot = jnp.einsum(
        "kgqj,qkgd->jkd", shifts, query_grid, preferred_element_type=jnp.float32
    ).reshape(key_window.shape[0], -1)
    value_cot = jnp.einsum(
        "kgqj,qkgd->jkd",
        weights.astype(jnp.bfloat16),
        grad_grid,
        preferred_element_type=jnp.float32,
    ).reshape(key_window.shape[0], -1)
    return (query_cot, key_cot, value_cot)


def per_device(hidden, query_weight, key_weight, value_weight, query_gain, key_gain, out_grad):
    token_count = out_grad.shape[0]
    group_size = HEADS // KV_HEADS
    block_rows = min(token_count, 512)
    block_count = token_count // block_rows
    window_rows = block_rows + WINDOW
    reach_blocks = (WINDOW - 2) // token_count + 1
    position_base = lax.axis_index("ctx") * token_count
    gathered = gather_over(hidden, "heads")
    query_proj = jnp.dot(gathered, query_weight, preferred_element_type=jnp.float32)
    key_proj = jnp.dot(gathered, key_weight, preferred_element_type=jnp.float32)
    value_proj = jnp.dot(gathered, value_weight, preferred_element_type=jnp.float32)
    positions = position_base + jnp.arange(token_count, dtype=jnp.int32)
    cosine, sine_table = rope_tables(positions, HEAD_DIM)
    query_full, query_back = jax.vjp(
        lambda projected: prepare(projected, cosine, sine_table, query_gain, SCALAR ** (-0.5)),
        query_proj,
    )
    key_full, key_back = jax.vjp(
        lambda projected: prepare(projected, cosine, sine_table, key_gain, 1.0), key_proj
    )
    query_cast = query_full.astype(jnp.bfloat16)
    key_value = jnp.stack([key_full.astype(jnp.bfloat16), value_proj.astype(jnp.bfloat16)])
    received = [passed_along(key_value, "ctx", distance) for distance in range(1, reach_blocks + 1)]
    window_pair = jnp.concatenate(received[::-1] + [key_value], axis=1)
    key_span = window_pair[0]
    value_span = window_pair[1]

    def window_of(block_index):
        block_start = block_index * block_rows
        query_pos = position_base + block_start + jnp.arange(block_rows, dtype=jnp.int32)
        key_pos = position_base - WINDOW + block_start + jnp.arange(window_rows, dtype=jnp.int32)
        return (query_cast, key_span, value_span, band_mask(query_pos, key_pos))

    def forward_block(block_index):
        query_block, key_window, value_window, allowed = window_of(block_index)
        return attend_forward(query_block, key_window, value_window, allowed, group_size)

    outputs, log_totals = lax.map(forward_block, jnp.arange(block_count, dtype=jnp.int32))
    attention = outputs.reshape(token_count, -1).astype(jnp.bfloat16)

    def backward_block(block_index, carry):
        query_acc, pair_acc = carry
        query_block, key_window, value_window, allowed = window_of(block_index)
        block_start = block_index * block_rows
        query_cot, key_cot, value_cot = attend_backward(
            query_block,
            key_window,
            value_window,
            allowed,
            log_totals[block_index],
            out_grad,
            attention,
            group_size,
        )
        query_acc = query_cot
        region = pair_acc + jnp.stack([key_cot, value_cot])
        pair_acc = region
        return (query_acc, pair_acc)

    query_zero = jnp.zeros((token_count, query_weight.shape[1]), jnp.float32)
    pair_zero = jnp.zeros((2, (reach_blocks + 1) * token_count, key_weight.shape[1]), jnp.float32)
    query_acc, pair_acc = lax.fori_loop(0, block_count, backward_block, (query_zero, pair_zero))
    grad_query = query_back(query_acc)[0].astype(jnp.bfloat16)
    grad_scale = float(lax.axis_size("ctx") * token_count) ** (-0.5)
    contract = (((0,), (0,)), ((), ()))
    own_pair = pair_acc[:, reach_blocks * token_count :]
    for distance in range(1, reach_blocks + 1):
        lower_row = (reach_blocks - distance) * token_count
        own_pair = own_pair + passed_along(
            pair_acc[:, lower_row : lower_row + token_count], "ctx", -distance
        )
    grad_key = key_back(own_pair[0])[0].astype(jnp.bfloat16)
    grad_value = own_pair[1].astype(jnp.bfloat16)
    key_width = key_weight.shape[1]
    query_width = query_weight.shape[1]
    summed = ctx_scatter_sum(
        lax.dot_general(
            gathered,
            jnp.concatenate([grad_query, grad_key, grad_value], axis=1),
            contract,
            preferred_element_type=jnp.float32,
        )
        * grad_scale,
        "ctx",
        (lax.axis_size("ctx") // 4, 2, 2),
    )
    query_weight_grad = summed[:, :query_width]
    key_weight_grad = summed[:, query_width : query_width + key_width]
    value_weight_grad = summed[:, query_width + key_width :]
    back_contract = (((1,), (1,)), ((), ()))
    partial_sum = lax.dot_general(
        grad_query, query_weight, back_contract, preferred_element_type=jnp.float32
    )
    partial_sum = partial_sum + lax.dot_general(
        grad_key, key_weight, back_contract, preferred_element_type=jnp.float32
    )
    input_grad = scatter_sum_over(
        (
            partial_sum
            + lax.dot_general(
                grad_value, value_weight, back_contract, preferred_element_type=jnp.float32
            )
        ).astype(jnp.bfloat16),
        "heads",
    ).astype(jnp.bfloat16)
    return (attention, input_grad, query_weight_grad, key_weight_grad, value_weight_grad)


def solution(mesh):
    return jax.shard_map(
        per_device,
        mesh=mesh,
        in_specs=(
            P(("ctx", "heads"), None),
            P(None, "heads"),
            P(None, "heads"),
            P(None, "heads"),
            P(),
            P(),
            P("ctx", "heads"),
        ),
        out_specs=(
            P("ctx", "heads"),
            P(("ctx", "heads"), None),
            P("ctx", "heads"),
            P("ctx", "heads"),
            P("ctx", "heads"),
        ),
        check_vma=False,
    )
```

```python
import math

import jax
import jax.numpy as jnp
from jax import lax
from jax.sharding import PartitionSpec as P

HEAD_DIM = 128
WINDOW = 1024
SCALAR = 168
HEADS = 16
KV_HEADS = 8


def passed_along(block, axis, distance):
    devices = range(lax.axis_size(axis))
    route = [(i - distance, i) for i in devices if i - distance in devices]
    return lax.ppermute(block, axis, route)


def torus_shifts(axis):
    size = lax.axis_size(axis)
    inner = size // 2 if size >= 4 else size
    outer = size // inner
    me = lax.axis_index(axis)

    def moved(index, dx, dy):
        return ((index // inner + dx) % outer) * inner + (index % inner + dy) % inner

    shifts = [(dx, dy) for dx in range(outer) for dy in range(inner)][1:]
    routes = [[(i, moved(i, dx, dy)) for i in range(size)] for dx, dy in shifts]
    targets = [moved(me, dx, dy) for dx, dy in shifts]
    slot_of = [
        ((me // inner - j // inner) % outer) * inner + (me % inner - j % inner) % inner
        for j in range(size)
    ]
    return (size, me, routes, targets, slot_of)


def gather_over(block, axis):
    size, me, routes, targets, slot_of = torus_shifts(axis)
    slots = jnp.stack([block] + [lax.ppermute(block, axis, route) for route in routes])
    order = jnp.stack([jnp.asarray(s, jnp.int32) for s in slot_of])
    return jnp.take(slots, order, axis=0).reshape((size * block.shape[0],) + block.shape[1:])


def scatter_sum_over(full, axis):
    size, me, routes, targets, slot_of = torus_shifts(axis)
    pieces = full.reshape((size, full.shape[0] // size) + full.shape[1:])
    total = lax.dynamic_index_in_dim(pieces, me, 0, keepdims=False).astype(jnp.float32)
    for route, target in zip(routes, targets):
        piece = lax.dynamic_index_in_dim(pieces, target, 0, keepdims=False)
        total = total + lax.ppermute(piece, axis, route).astype(jnp.float32)
    return total


def ring_scatter_sum(blocks, axis, count, stride, forward):
    size = lax.axis_size(axis)
    me = lax.axis_index(axis)
    digit = (me // stride) % count
    step = 1 if forward else -1
    route = [
        (i, i - ((i // stride) % count) * stride + (((i // stride) % count + step) % count) * stride)
        for i in range(size)
    ]

    def chunk(k):
        return lax.dynamic_index_in_dim(blocks, (digit - step * (k + 1)) % count, 0, keepdims=False)

    running = chunk(0)
    for k in range(count - 1):
        running = lax.ppermute(running.astype(jnp.bfloat16), axis, route).astype(jnp.float32) + chunk(k + 1)
    return running


def pair_scatter_sum(blocks, axis, stride):
    size = lax.axis_size(axis)
    me = lax.axis_index(axis)
    digit = (me // stride) % 2
    route = [(i, i + stride if (i // stride) % 2 == 0 else i - stride) for i in range(size)]
    own = lax.dynamic_index_in_dim(blocks, digit, 0, keepdims=False)
    other = lax.dynamic_index_in_dim(blocks, 1 - digit, 0, keepdims=False)
    return own + lax.ppermute(other.astype(jnp.bfloat16), axis, route).astype(jnp.float32)


def ctx_scatter_sum(full, axis, levels):
    outer, middle, inner = levels
    width = full.shape[1]
    grid = full.reshape(outer, middle, inner, -1, width)
    grid = jnp.moveaxis(grid, 2, 0)
    grid = pair_scatter_sum(grid, axis, 1)
    half = width // 2
    up = ring_scatter_sum(grid[..., :half], axis, outer, middle * inner, True)
    down = ring_scatter_sum(grid[..., half:], axis, outer, middle * inner, False)
    grid = jnp.concatenate([up, down], axis=-1)
    return pair_scatter_sum(grid, axis, inner)


def gather_all(block, axis):
    size = lax.axis_size(axis)
    copies = jnp.broadcast_to(block[None], (size,) + block.shape)
    received = lax.all_to_all(copies, axis, 0, 0)
    return received.reshape((size * block.shape[0],) + block.shape[1:])


def exchange_sum(full, axis):
    size = lax.axis_size(axis)
    pieces = full.reshape((size, full.shape[0] // size) + full.shape[1:])
    received = lax.all_to_all(pieces, axis, 0, 0)
    return jnp.sum(received.astype(jnp.float32), axis=0)


def rope_tables(positions, head_size):
    half_size = head_size // 2
    indices = jnp.arange(half_size, dtype=jnp.float32)
    inverse = jnp.exp(indices * (-2.0 * math.log(10000.0) / head_size))
    angles = positions.astype(jnp.float32)[:, None] * inverse[None, :]
    return (jnp.cos(angles), jnp.sin(angles))


def prepare(projected, cosine, sine_table, channel_gain, factor):
    row_count = projected.shape[0]
    head_size = channel_gain.shape[0]
    pieces = projected.reshape(row_count, -1, head_size)
    normed = (
        pieces * lax.rsqrt(jnp.mean(pieces * pieces, axis=-1, keepdims=True) + 1e-06) * channel_gain
    )
    half_size = head_size // 2
    leading = normed[..., :half_size]
    trailing = normed[..., half_size:]
    cos_rows = cosine[:, None, :]
    sin_rows = sine_table[:, None, :]
    turned = jnp.concatenate(
        [leading * cos_rows - trailing * sin_rows, trailing * cos_rows + leading * sin_rows],
        axis=-1,
    )
    return (turned * factor).reshape(row_count, -1)


def band_mask(query_pos, key_pos):
    separation = query_pos[:, None] - key_pos[None, :]
    return (separation >= 0) & (separation < WINDOW) & (key_pos[None, :] >= 0)


def head_grids(query_block, key_window, value_window, group_size):
    query_grid = query_block.reshape(query_block.shape[0], -1, group_size, HEAD_DIM)
    key_grid = key_window.reshape(key_window.shape[0], -1, HEAD_DIM)
    value_grid = value_window.reshape(value_window.shape[0], -1, HEAD_DIM)
    return (query_grid, key_grid, value_grid)


def attend_forward(query_block, key_window, value_window, allowed, group_size):
    query_grid, key_grid, value_grid = head_grids(query_block, key_window, value_window, group_size)
    scores = jnp.einsum("qkgd,jkd->kgqj", query_grid, key_grid, preferred_element_type=jnp.float32)
    masked = jnp.where(allowed, scores, -1e30)
    highest = jnp.max(masked, axis=-1, keepdims=True)
    total = jnp.sum(jnp.exp(masked - highest), axis=-1, keepdims=True)
    log_total = highest + jnp.log(total)
    weights = jnp.where(allowed, jnp.exp(masked - log_total), 0.0)
    output = jnp.einsum(
        "kgqj,jkd->qkgd",
        weights.astype(jnp.bfloat16),
        value_grid,
        preferred_element_type=jnp.float32,
    )
    return (output.reshape(query_block.shape[0], -1), log_total[..., 0])


def attend_backward(
    query_block,
    key_window,
    value_window,
    allowed,
    log_total,
    out_block,
    attention_block,
    group_size,
):
    query_grid, key_grid, value_grid = head_grids(query_block, key_window, value_window, group_size)
    row_count = query_block.shape[0]
    grad_grid = out_block.reshape(row_count, -1, group_size, HEAD_DIM)
    attention_grid = attention_block.reshape(row_count, -1, group_size, HEAD_DIM)
    scores = jnp.einsum("qkgd,jkd->kgqj", query_grid, key_grid, preferred_element_type=jnp.float32)
    masked = jnp.where(allowed, scores, -1e30)
    weights = jnp.where(allowed, jnp.exp(masked - log_total[..., None]), 0.0)
    delta = jnp.einsum(
        "qkgd,qkgd->kgq", grad_grid, attention_grid, preferred_element_type=jnp.float32
    )
    products = jnp.einsum(
        "qkgd,jkd->kgqj", grad_grid, value_grid, preferred_element_type=jnp.float32
    )
    shifts = (weights * (products - delta[..., None])).astype(jnp.bfloat16)
    query_cot = jnp.einsum(
        "kgqj,jkd->qkgd", shifts, key_grid, preferred_element_type=jnp.float32
    ).reshape(row_count, -1)
    key_cot = jnp.einsum(
        "kgqj,qkgd->jkd", shifts, query_grid, preferred_element_type=jnp.float32
    ).reshape(key_window.shape[0], -1)
    value_cot = jnp.einsum(
        "kgqj,qkgd->jkd",
        weights.astype(jnp.bfloat16),
        grad_grid,
        preferred_element_type=jnp.float32,
    ).reshape(key_window.shape[0], -1)
    return (query_cot, key_cot, value_cot)


def per_device(hidden, query_weight, key_weight, value_weight, query_gain, key_gain, out_grad):
    token_count = out_grad.shape[0]
    group_size = HEADS // KV_HEADS
    block_rows = min(token_count, 512)
    block_count = token_count // block_rows
    window_rows = block_rows + WINDOW
    reach_blocks = (WINDOW - 2) // token_count + 1
    position_base = lax.axis_index("ctx") * token_count
    gathered = gather_all(hidden, "heads")
    query_proj = jnp.dot(gathered, query_weight, preferred_element_type=jnp.float32)
    key_proj = jnp.dot(gathered, key_weight, preferred_element_type=jnp.float32)
    value_proj = jnp.dot(gathered, value_weight, preferred_element_type=jnp.float32)
    positions = position_base + jnp.arange(token_count, dtype=jnp.int32)
    cosine, sine_table = rope_tables(positions, HEAD_DIM)
    query_full, query_back = jax.vjp(
        lambda projected: prepare(projected, cosine, sine_table, query_gain, SCALAR ** (-0.5)),
        query_proj,
    )
    key_full, key_back = jax.vjp(
        lambda projected: prepare(projected, cosine, sine_table, key_gain, 1.0), key_proj
    )
    query_cast = query_full.astype(jnp.bfloat16)
    key_value = jnp.stack([key_full.astype(jnp.bfloat16), value_proj.astype(jnp.bfloat16)])
    received = [passed_along(key_value, "ctx", distance) for distance in range(1, reach_blocks + 1)]
    window_pair = jnp.concatenate(received[::-1] + [key_value], axis=1)
    key_span = window_pair[0]
    value_span = window_pair[1]

    def window_of(block_index):
        block_start = block_index * block_rows
        query_pos = position_base + block_start + jnp.arange(block_rows, dtype=jnp.int32)
        key_pos = position_base - WINDOW + block_start + jnp.arange(window_rows, dtype=jnp.int32)
        return (query_cast, key_span, value_span, band_mask(query_pos, key_pos))

    def forward_block(block_index):
        query_block, key_window, value_window, allowed = window_of(block_index)
        return attend_forward(query_block, key_window, value_window, allowed, group_size)

    outputs, log_totals = lax.map(forward_block, jnp.arange(block_count, dtype=jnp.int32))
    attention = outputs.reshape(token_count, -1).astype(jnp.bfloat16)

    def backward_block(block_index, carry):
        query_acc, pair_acc = carry
        query_block, key_window, value_window, allowed = window_of(block_index)
        block_start = block_index * block_rows
        query_cot, key_cot, value_cot = attend_backward(
            query_block,
            key_window,
            value_window,
            allowed,
            log_totals[block_index],
            out_grad,
            attention,
            group_size,
        )
        query_acc = query_cot
        region = pair_acc + jnp.stack([key_cot, value_cot])
        pair_acc = region
        return (query_acc, pair_acc)

    query_zero = jnp.zeros((token_count, query_weight.shape[1]), jnp.float32)
    pair_zero = jnp.zeros((2, (reach_blocks + 1) * token_count, key_weight.shape[1]), jnp.float32)
    query_acc, pair_acc = lax.fori_loop(0, block_count, backward_block, (query_zero, pair_zero))
    grad_query = query_back(query_acc)[0].astype(jnp.bfloat16)
    grad_scale = float(lax.axis_size("ctx") * token_count) ** (-0.5)
    contract = (((0,), (0,)), ((), ()))
    own_pair = pair_acc[:, reach_blocks * token_count :]
    for distance in range(1, reach_blocks + 1):
        lower_row = (reach_blocks - distance) * token_count
        own_pair = own_pair + passed_along(
            pair_acc[:, lower_row : lower_row + token_count], "ctx", -distance
        )
    grad_key = key_back(own_pair[0])[0].astype(jnp.bfloat16)
    grad_value = own_pair[1].astype(jnp.bfloat16)
    key_width = key_weight.shape[1]
    query_width = query_weight.shape[1]
    summed = ctx_scatter_sum(
        lax.dot_general(
            gathered,
            jnp.concatenate([grad_query, grad_key, grad_value], axis=1),
            contract,
            preferred_element_type=jnp.float32,
        )
        * grad_scale,
        "ctx",
        (lax.axis_size("ctx") // 4, 2, 2),
    )
    query_weight_grad = summed[:, :query_width]
    key_weight_grad = summed[:, query_width : query_width + key_width]
    value_weight_grad = summed[:, query_width + key_width :]
    back_contract = (((1,), (1,)), ((), ()))
    partial_sum = lax.dot_general(
        grad_query, query_weight, back_contract, preferred_element_type=jnp.float32
    )
    partial_sum = partial_sum + lax.dot_general(
        grad_key, key_weight, back_contract, preferred_element_type=jnp.float32
    )
    input_grad = exchange_sum(
        (
            partial_sum
            + lax.dot_general(
                grad_value, value_weight, back_contract, preferred_element_type=jnp.float32
            )
        ).astype(jnp.bfloat16),
        "heads",
    ).astype(jnp.bfloat16)
    return (attention, input_grad, query_weight_grad, key_weight_grad, value_weight_grad)


def solution(mesh):
    return jax.shard_map(
        per_device,
        mesh=mesh,
        in_specs=(
            P(("ctx", "heads"), None),
            P(None, "heads"),
            P(None, "heads"),
            P(None, "heads"),
            P(),
            P(),
            P("ctx", "heads"),
        ),
        out_specs=(
            P("ctx", "heads"),
            P(("ctx", "heads"), None),
            P("ctx", "heads"),
            P("ctx", "heads"),
            P("ctx", "heads"),
        ),
        check_vma=False,
    )
```

```python
import math

import jax
import jax.numpy as jnp
from jax import lax
from jax.sharding import PartitionSpec as P

HEAD_DIM = 128
WINDOW = 1024
SCALAR = 168
HEADS = 16
KV_HEADS = 8


def passed_along(block, axis, distance):
    devices = range(lax.axis_size(axis))
    route = [(i - distance, i) for i in devices if i - distance in devices]
    return lax.ppermute(block, axis, route)


def torus_shifts(axis):
    size = lax.axis_size(axis)
    inner = size // 2 if size >= 4 else size
    outer = size // inner
    me = lax.axis_index(axis)

    def moved(index, dx, dy):
        return ((index // inner + dx) % outer) * inner + (index % inner + dy) % inner

    shifts = [(dx, dy) for dx in range(outer) for dy in range(inner)][1:]
    routes = [[(i, moved(i, dx, dy)) for i in range(size)] for dx, dy in shifts]
    targets = [moved(me, dx, dy) for dx, dy in shifts]
    slot_of = [
        ((me // inner - j // inner) % outer) * inner + (me % inner - j % inner) % inner
        for j in range(size)
    ]
    return (size, me, routes, targets, slot_of)


def gather_over(block, axis):
    size, me, routes, targets, slot_of = torus_shifts(axis)
    slots = jnp.stack([block] + [lax.ppermute(block, axis, route) for route in routes])
    order = jnp.stack([jnp.asarray(s, jnp.int32) for s in slot_of])
    return jnp.take(slots, order, axis=0).reshape((size * block.shape[0],) + block.shape[1:])


def scatter_sum_over(full, axis):
    size, me, routes, targets, slot_of = torus_shifts(axis)
    pieces = full.reshape((size, full.shape[0] // size) + full.shape[1:])
    total = lax.dynamic_index_in_dim(pieces, me, 0, keepdims=False).astype(jnp.float32)
    for route, target in zip(routes, targets):
        piece = lax.dynamic_index_in_dim(pieces, target, 0, keepdims=False)
        total = total + lax.ppermute(piece, axis, route).astype(jnp.float32)
    return total


def ring_scatter_sum(blocks, axis, count, stride, forward):
    size = lax.axis_size(axis)
    me = lax.axis_index(axis)
    digit = (me // stride) % count
    step = 1 if forward else -1
    route = [
        (i, i - ((i // stride) % count) * stride + (((i // stride) % count + step) % count) * stride)
        for i in range(size)
    ]

    def chunk(k):
        return lax.dynamic_index_in_dim(blocks, (digit - step * (k + 1)) % count, 0, keepdims=False)

    running = chunk(0)
    for k in range(count - 1):
        running = lax.ppermute(running.astype(jnp.bfloat16), axis, route).astype(jnp.float32) + chunk(k + 1)
    return running


def pair_scatter_sum(blocks, axis, stride):
    size = lax.axis_size(axis)
    me = lax.axis_index(axis)
    digit = (me // stride) % 2
    route = [(i, i + stride if (i // stride) % 2 == 0 else i - stride) for i in range(size)]
    own = lax.dynamic_index_in_dim(blocks, digit, 0, keepdims=False).astype(jnp.float32)
    other = lax.dynamic_index_in_dim(blocks, 1 - digit, 0, keepdims=False)
    return own + lax.ppermute(other.astype(jnp.bfloat16), axis, route).astype(jnp.float32)


def ctx_scatter_sum(full, axis, levels):
    outer, middle, inner = levels
    width = full.shape[1]
    grid = full.reshape(outer, middle, inner, -1, width)
    grid = jnp.moveaxis(grid, 2, 0)
    grid = pair_scatter_sum(grid, axis, 1)
    half = width // 2
    up = ring_scatter_sum(grid[..., :half], axis, outer, middle * inner, True)
    down = ring_scatter_sum(grid[..., half:], axis, outer, middle * inner, False)
    grid = jnp.concatenate([up, down], axis=-1)
    return pair_scatter_sum(grid, axis, inner)


def gather_all(block, axis):
    size = lax.axis_size(axis)
    copies = jnp.broadcast_to(block[None], (size,) + block.shape)
    received = lax.all_to_all(copies, axis, 0, 0)
    return received.reshape((size * block.shape[0],) + block.shape[1:])


def exchange_sum(full, axis):
    size = lax.axis_size(axis)
    pieces = full.reshape((size, full.shape[0] // size) + full.shape[1:])
    received = lax.all_to_all(pieces, axis, 0, 0)
    return jnp.sum(received.astype(jnp.float32), axis=0)


def rope_tables(positions, head_size):
    half_size = head_size // 2
    indices = jnp.arange(half_size, dtype=jnp.float32)
    inverse = jnp.exp(indices * (-2.0 * math.log(10000.0) / head_size))
    angles = positions.astype(jnp.float32)[:, None] * inverse[None, :]
    return (jnp.cos(angles), jnp.sin(angles))


def prepare(projected, cosine, sine_table, channel_gain, factor):
    row_count = projected.shape[0]
    head_size = channel_gain.shape[0]
    pieces = projected.reshape(row_count, -1, head_size)
    normed = (
        pieces * lax.rsqrt(jnp.mean(pieces * pieces, axis=-1, keepdims=True) + 1e-06) * channel_gain
    )
    half_size = head_size // 2
    leading = normed[..., :half_size]
    trailing = normed[..., half_size:]
    cos_rows = cosine[:, None, :]
    sin_rows = sine_table[:, None, :]
    turned = jnp.concatenate(
        [leading * cos_rows - trailing * sin_rows, trailing * cos_rows + leading * sin_rows],
        axis=-1,
    )
    return (turned * factor).reshape(row_count, -1)


def band_mask(query_pos, key_pos):
    separation = query_pos[:, None] - key_pos[None, :]
    return (separation >= 0) & (separation < WINDOW) & (key_pos[None, :] >= 0)


def head_grids(query_block, key_window, value_window, group_size):
    query_grid = query_block.reshape(query_block.shape[0], -1, group_size, HEAD_DIM)
    key_grid = key_window.reshape(key_window.shape[0], -1, HEAD_DIM)
    value_grid = value_window.reshape(value_window.shape[0], -1, HEAD_DIM)
    return (query_grid, key_grid, value_grid)


def attend_forward(query_block, key_window, value_window, allowed, group_size):
    query_grid, key_grid, value_grid = head_grids(query_block, key_window, value_window, group_size)
    scores = jnp.einsum("qkgd,jkd->kgqj", query_grid, key_grid, preferred_element_type=jnp.float32)
    masked = jnp.where(allowed, scores, -1e30)
    highest = jnp.max(masked, axis=-1, keepdims=True)
    total = jnp.sum(jnp.exp(masked - highest), axis=-1, keepdims=True)
    log_total = highest + jnp.log(total)
    weights = jnp.where(allowed, jnp.exp(masked - log_total), 0.0)
    output = jnp.einsum(
        "kgqj,jkd->qkgd",
        weights.astype(jnp.bfloat16),
        value_grid,
        preferred_element_type=jnp.float32,
    )
    return (output.reshape(query_block.shape[0], -1), log_total[..., 0])


def attend_backward(
    query_block,
    key_window,
    value_window,
    allowed,
    log_total,
    out_block,
    attention_block,
    group_size,
):
    query_grid, key_grid, value_grid = head_grids(query_block, key_window, value_window, group_size)
    row_count = query_block.shape[0]
    grad_grid = out_block.reshape(row_count, -1, group_size, HEAD_DIM)
    attention_grid = attention_block.reshape(row_count, -1, group_size, HEAD_DIM)
    scores = jnp.einsum("qkgd,jkd->kgqj", query_grid, key_grid, preferred_element_type=jnp.float32)
    masked = jnp.where(allowed, scores, -1e30)
    weights = jnp.where(allowed, jnp.exp(masked - log_total[..., None]), 0.0)
    delta = jnp.einsum(
        "qkgd,qkgd->kgq", grad_grid, attention_grid, preferred_element_type=jnp.float32
    )
    products = jnp.einsum(
        "qkgd,jkd->kgqj", grad_grid, value_grid, preferred_element_type=jnp.float32
    )
    shifts = (weights * (products - delta[..., None])).astype(jnp.bfloat16)
    query_cot = jnp.einsum(
        "kgqj,jkd->qkgd", shifts, key_grid, preferred_element_type=jnp.float32
    ).reshape(row_count, -1)
    key_cot = jnp.einsum(
        "kgqj,qkgd->jkd", shifts, query_grid, preferred_element_type=jnp.float32
    ).reshape(key_window.shape[0], -1)
    value_cot = jnp.einsum(
        "kgqj,qkgd->jkd",
        weights.astype(jnp.bfloat16),
        grad_grid,
        preferred_element_type=jnp.float32,
    ).reshape(key_window.shape[0], -1)
    return (query_cot, key_cot, value_cot)


def per_device(hidden, query_weight, key_weight, value_weight, query_gain, key_gain, out_grad):
    token_count = out_grad.shape[0]
    group_size = HEADS // KV_HEADS
    block_rows = min(token_count, 512)
    block_count = token_count // block_rows
    window_rows = block_rows + WINDOW
    reach_blocks = (WINDOW - 2) // token_count + 1
    position_base = lax.axis_index("ctx") * token_count
    gathered = gather_all(hidden, "heads")
    query_width = query_weight.shape[1]
    key_width = key_weight.shape[1]
    weight_cat = jnp.concatenate([query_weight, key_weight, value_weight], axis=1)
    projected = jnp.dot(gathered, weight_cat, preferred_element_type=jnp.float32)
    query_proj = projected[:, :query_width]
    key_proj = projected[:, query_width : query_width + key_width]
    value_proj = projected[:, query_width + key_width :]
    positions = position_base + jnp.arange(token_count, dtype=jnp.int32)
    cosine, sine_table = rope_tables(positions, HEAD_DIM)
    query_full, query_back = jax.vjp(
        lambda projected: prepare(projected, cosine, sine_table, query_gain, SCALAR ** (-0.5)),
        query_proj,
    )
    key_full, key_back = jax.vjp(
        lambda projected: prepare(projected, cosine, sine_table, key_gain, 1.0), key_proj
    )
    query_cast = query_full.astype(jnp.bfloat16)
    key_value = jnp.stack([key_full.astype(jnp.bfloat16), value_proj.astype(jnp.bfloat16)])
    received = [passed_along(key_value, "ctx", distance) for distance in range(1, reach_blocks + 1)]
    window_pair = jnp.concatenate(received[::-1] + [key_value], axis=1)
    key_span = window_pair[0]
    value_span = window_pair[1]

    def window_of(block_index):
        block_start = block_index * block_rows
        query_pos = position_base + block_start + jnp.arange(block_rows, dtype=jnp.int32)
        key_pos = position_base - WINDOW + block_start + jnp.arange(window_rows, dtype=jnp.int32)
        return (query_cast, key_span, value_span, band_mask(query_pos, key_pos))

    def forward_block(block_index):
        query_block, key_window, value_window, allowed = window_of(block_index)
        return attend_forward(query_block, key_window, value_window, allowed, group_size)

    outputs, log_totals = lax.map(forward_block, jnp.arange(block_count, dtype=jnp.int32))
    attention = outputs.reshape(token_count, -1).astype(jnp.bfloat16)

    def backward_block(block_index, carry):
        query_acc, pair_acc = carry
        query_block, key_window, value_window, allowed = window_of(block_index)
        block_start = block_index * block_rows
        query_cot, key_cot, value_cot = attend_backward(
            query_block,
            key_window,
            value_window,
            allowed,
            log_totals[block_index],
            out_grad,
            attention,
            group_size,
        )
        query_acc = query_cot
        region = pair_acc + jnp.stack([key_cot, value_cot])
        pair_acc = region
        return (query_acc, pair_acc)

    query_zero = jnp.zeros((token_count, query_weight.shape[1]), jnp.float32)
    pair_zero = jnp.zeros((2, (reach_blocks + 1) * token_count, key_weight.shape[1]), jnp.float32)
    query_acc, pair_acc = lax.fori_loop(0, block_count, backward_block, (query_zero, pair_zero))
    grad_query = query_back(query_acc)[0].astype(jnp.bfloat16)
    grad_scale = float(lax.axis_size("ctx") * token_count) ** (-0.5)
    contract = (((0,), (0,)), ((), ()))
    own_pair = pair_acc[:, reach_blocks * token_count :]
    for distance in range(1, reach_blocks + 1):
        lower_row = (reach_blocks - distance) * token_count
        own_pair = own_pair + passed_along(
            pair_acc[:, lower_row : lower_row + token_count], "ctx", -distance
        )
    grad_key = key_back(own_pair[0])[0].astype(jnp.bfloat16)
    grad_value = own_pair[1].astype(jnp.bfloat16)
    grad_cat = jnp.concatenate([grad_query, grad_key, grad_value], axis=1)
    summed = ctx_scatter_sum(
        (
            lax.dot_general(gathered, grad_cat, contract, preferred_element_type=jnp.float32)
            * grad_scale
        ).astype(jnp.bfloat16),
        "ctx",
        (lax.axis_size("ctx") // 4, 2, 2),
    )
    query_weight_grad = summed[:, :query_width]
    key_weight_grad = summed[:, query_width : query_width + key_width]
    value_weight_grad = summed[:, query_width + key_width :]
    back_contract = (((1,), (1,)), ((), ()))
    input_grad = exchange_sum(
        lax.dot_general(
            grad_cat, weight_cat, back_contract, preferred_element_type=jnp.float32
        ).astype(jnp.bfloat16),
        "heads",
    ).astype(jnp.bfloat16)
    return (attention, input_grad, query_weight_grad, key_weight_grad, value_weight_grad)


def solution(mesh):
    return jax.shard_map(
        per_device,
        mesh=mesh,
        in_specs=(
            P(("ctx", "heads"), None),
            P(None, "heads"),
            P(None, "heads"),
            P(None, "heads"),
            P(),
            P(),
            P("ctx", "heads"),
        ),
        out_specs=(
            P("ctx", "heads"),
            P(("ctx", "heads"), None),
            P("ctx", "heads"),
            P("ctx", "heads"),
            P("ctx", "heads"),
        ),
        check_vma=False,
    )
```

```python
import math

import jax
import jax.numpy as jnp
from jax import lax
from jax.sharding import PartitionSpec as P

HEAD_DIM = 128
WINDOW = 1024
SCALAR = 168
HEADS = 16
KV_HEADS = 8


def passed_along(block, axis, distance):
    devices = range(lax.axis_size(axis))
    route = [(i - distance, i) for i in devices if i - distance in devices]
    return lax.ppermute(block, axis, route)


def torus_shifts(axis):
    size = lax.axis_size(axis)
    inner = size // 2 if size >= 4 else size
    outer = size // inner
    me = lax.axis_index(axis)

    def moved(index, dx, dy):
        return ((index // inner + dx) % outer) * inner + (index % inner + dy) % inner

    shifts = [(dx, dy) for dx in range(outer) for dy in range(inner)][1:]
    routes = [[(i, moved(i, dx, dy)) for i in range(size)] for dx, dy in shifts]
    targets = [moved(me, dx, dy) for dx, dy in shifts]
    slot_of = [
        ((me // inner - j // inner) % outer) * inner + (me % inner - j % inner) % inner
        for j in range(size)
    ]
    return (size, me, routes, targets, slot_of)


def gather_over(block, axis):
    size, me, routes, targets, slot_of = torus_shifts(axis)
    slots = jnp.stack([block] + [lax.ppermute(block, axis, route) for route in routes])
    order = jnp.stack([jnp.asarray(s, jnp.int32) for s in slot_of])
    return jnp.take(slots, order, axis=0).reshape((size * block.shape[0],) + block.shape[1:])


def scatter_sum_over(full, axis):
    size, me, routes, targets, slot_of = torus_shifts(axis)
    pieces = full.reshape((size, full.shape[0] // size) + full.shape[1:])
    total = lax.dynamic_index_in_dim(pieces, me, 0, keepdims=False).astype(jnp.float32)
    for route, target in zip(routes, targets):
        piece = lax.dynamic_index_in_dim(pieces, target, 0, keepdims=False)
        total = total + lax.ppermute(piece, axis, route).astype(jnp.float32)
    return total


def ring_scatter_sum(blocks, axis, count, stride):
    size = lax.axis_size(axis)
    me = lax.axis_index(axis)
    digit = (me // stride) % count
    half = blocks.shape[-1] // 2

    def route(step):
        return [
            (i, i - ((i // stride) % count) * stride + (((i // stride) % count + step) % count) * stride)
            for i in range(size)
        ]

    def chunk(k, step, lo):
        block = lax.dynamic_index_in_dim(blocks, (digit - step * (k + 1)) % count, 0, keepdims=False)
        return block[..., lo : lo + half]

    def advance(k, carry):
        up, down = carry
        up = lax.ppermute(up.astype(jnp.bfloat16), axis, route(1)).astype(jnp.float32)
        down = lax.ppermute(down.astype(jnp.bfloat16), axis, route(-1)).astype(jnp.float32)
        return (up + chunk(k + 1, 1, 0), down + chunk(k + 1, -1, half))

    up, down = lax.fori_loop(0, count - 1, advance, (chunk(0, 1, 0), chunk(0, -1, half)))
    return jnp.concatenate([up, down], axis=-1)


def pair_scatter_sum(blocks, axis, stride):
    size = lax.axis_size(axis)
    me = lax.axis_index(axis)
    digit = (me // stride) % 2
    route = [(i, i + stride if (i // stride) % 2 == 0 else i - stride) for i in range(size)]
    own = lax.dynamic_index_in_dim(blocks, digit, 0, keepdims=False).astype(jnp.float32)
    other = lax.dynamic_index_in_dim(blocks, 1 - digit, 0, keepdims=False)
    return own + lax.ppermute(other.astype(jnp.bfloat16), axis, route).astype(jnp.float32)


def ctx_scatter_sum(full, axis, levels):
    outer, middle, inner = levels
    width = full.shape[1]
    grid = full.reshape(outer, middle, inner, -1, width)
    grid = jnp.moveaxis(grid, 2, 0)
    grid = pair_scatter_sum(grid, axis, 1)
    grid = ring_scatter_sum(grid, axis, outer, middle * inner)
    return pair_scatter_sum(grid, axis, inner)


def gather_all(block, axis):
    size = lax.axis_size(axis)
    copies = jnp.broadcast_to(block[None], (size,) + block.shape)
    received = lax.all_to_all(copies, axis, 0, 0)
    return received.reshape((size * block.shape[0],) + block.shape[1:])


def exchange_sum(full, axis):
    size = lax.axis_size(axis)
    pieces = full.reshape((size, full.shape[0] // size) + full.shape[1:])
    received = lax.all_to_all(pieces, axis, 0, 0)
    return jnp.sum(received.astype(jnp.float32), axis=0)


def rope_tables(positions, head_size):
    half_size = head_size // 2
    indices = jnp.arange(half_size, dtype=jnp.float32)
    inverse = jnp.exp(indices * (-2.0 * math.log(10000.0) / head_size))
    angles = positions.astype(jnp.float32)[:, None] * inverse[None, :]
    return (jnp.cos(angles), jnp.sin(angles))


def prepare(projected, cosine, sine_table, channel_gain, factor):
    row_count = projected.shape[0]
    head_size = channel_gain.shape[0]
    pieces = projected.reshape(row_count, -1, head_size)
    normed = (
        pieces * lax.rsqrt(jnp.mean(pieces * pieces, axis=-1, keepdims=True) + 1e-06) * channel_gain
    )
    half_size = head_size // 2
    leading = normed[..., :half_size]
    trailing = normed[..., half_size:]
    cos_rows = cosine[:, None, :]
    sin_rows = sine_table[:, None, :]
    turned = jnp.concatenate(
        [leading * cos_rows - trailing * sin_rows, trailing * cos_rows + leading * sin_rows],
        axis=-1,
    )
    return (turned * factor).reshape(row_count, -1)


def band_mask(query_pos, key_pos):
    separation = query_pos[:, None] - key_pos[None, :]
    return (separation >= 0) & (separation < WINDOW) & (key_pos[None, :] >= 0)


def head_grids(query_block, key_window, value_window, group_size):
    query_grid = query_block.reshape(query_block.shape[0], -1, group_size, HEAD_DIM)
    key_grid = key_window.reshape(key_window.shape[0], -1, HEAD_DIM)
    value_grid = value_window.reshape(value_window.shape[0], -1, HEAD_DIM)
    return (query_grid, key_grid, value_grid)


def attend_forward(query_block, key_window, value_window, allowed, group_size):
    query_grid, key_grid, value_grid = head_grids(query_block, key_window, value_window, group_size)
    scores = jnp.einsum("qkgd,jkd->kgqj", query_grid, key_grid, preferred_element_type=jnp.float32)
    masked = jnp.where(allowed, scores, -1e30)
    highest = jnp.max(masked, axis=-1, keepdims=True)
    total = jnp.sum(jnp.exp(masked - highest), axis=-1, keepdims=True)
    log_total = highest + jnp.log(total)
    weights = jnp.where(allowed, jnp.exp(masked - log_total), 0.0)
    output = jnp.einsum(
        "kgqj,jkd->qkgd",
        weights.astype(jnp.bfloat16),
        value_grid,
        preferred_element_type=jnp.float32,
    )
    return (output.reshape(query_block.shape[0], -1), log_total[..., 0])


def attend_backward(
    query_block,
    key_window,
    value_window,
    allowed,
    log_total,
    out_block,
    attention_block,
    group_size,
):
    query_grid, key_grid, value_grid = head_grids(query_block, key_window, value_window, group_size)
    row_count = query_block.shape[0]
    grad_grid = out_block.reshape(row_count, -1, group_size, HEAD_DIM)
    attention_grid = attention_block.reshape(row_count, -1, group_size, HEAD_DIM)
    scores = jnp.einsum("qkgd,jkd->kgqj", query_grid, key_grid, preferred_element_type=jnp.float32)
    masked = jnp.where(allowed, scores, -1e30)
    weights = jnp.where(allowed, jnp.exp(masked - log_total[..., None]), 0.0)
    delta = jnp.einsum(
        "qkgd,qkgd->kgq", grad_grid, attention_grid, preferred_element_type=jnp.float32
    )
    products = jnp.einsum(
        "qkgd,jkd->kgqj", grad_grid, value_grid, preferred_element_type=jnp.float32
    )
    shifts = (weights * (products - delta[..., None])).astype(jnp.bfloat16)
    query_cot = jnp.einsum(
        "kgqj,jkd->qkgd", shifts, key_grid, preferred_element_type=jnp.float32
    ).reshape(row_count, -1)
    key_cot = jnp.einsum(
        "kgqj,qkgd->jkd", shifts, query_grid, preferred_element_type=jnp.float32
    ).reshape(key_window.shape[0], -1)
    value_cot = jnp.einsum(
        "kgqj,qkgd->jkd",
        weights.astype(jnp.bfloat16),
        grad_grid,
        preferred_element_type=jnp.float32,
    ).reshape(key_window.shape[0], -1)
    return (query_cot, key_cot, value_cot)


def per_device(hidden, query_weight, key_weight, value_weight, query_gain, key_gain, out_grad):
    token_count = out_grad.shape[0]
    group_size = HEADS // KV_HEADS
    block_rows = min(token_count, 512)
    block_count = token_count // block_rows
    window_rows = block_rows + WINDOW
    reach_blocks = (WINDOW - 2) // token_count + 1
    position_base = lax.axis_index("ctx") * token_count
    gathered = gather_all(hidden, "heads")
    query_width = query_weight.shape[1]
    key_width = key_weight.shape[1]
    weight_cat = jnp.concatenate([query_weight, key_weight, value_weight], axis=1)
    projected = jnp.dot(gathered, weight_cat, preferred_element_type=jnp.float32)
    query_proj = projected[:, :query_width]
    key_proj = projected[:, query_width : query_width + key_width]
    value_proj = projected[:, query_width + key_width :]
    positions = position_base + jnp.arange(token_count, dtype=jnp.int32)
    cosine, sine_table = rope_tables(positions, HEAD_DIM)
    query_full, query_back = jax.vjp(
        lambda projected: prepare(projected, cosine, sine_table, query_gain, SCALAR ** (-0.5)),
        query_proj,
    )
    key_full, key_back = jax.vjp(
        lambda projected: prepare(projected, cosine, sine_table, key_gain, 1.0), key_proj
    )
    query_cast = query_full.astype(jnp.bfloat16)
    key_value = jnp.stack([key_full.astype(jnp.bfloat16), value_proj.astype(jnp.bfloat16)])
    received = [passed_along(key_value, "ctx", distance) for distance in range(1, reach_blocks + 1)]
    window_pair = jnp.concatenate(received[::-1] + [key_value], axis=1)
    key_span = window_pair[0]
    value_span = window_pair[1]

    def window_of(block_index):
        block_start = block_index * block_rows
        query_pos = position_base + block_start + jnp.arange(block_rows, dtype=jnp.int32)
        key_pos = position_base - WINDOW + block_start + jnp.arange(window_rows, dtype=jnp.int32)
        return (query_cast, key_span, value_span, band_mask(query_pos, key_pos))

    def forward_block(block_index):
        query_block, key_window, value_window, allowed = window_of(block_index)
        return attend_forward(query_block, key_window, value_window, allowed, group_size)

    outputs, log_totals = lax.map(forward_block, jnp.arange(block_count, dtype=jnp.int32))
    attention = outputs.reshape(token_count, -1).astype(jnp.bfloat16)

    def backward_block(block_index, carry):
        query_acc, pair_acc = carry
        query_block, key_window, value_window, allowed = window_of(block_index)
        block_start = block_index * block_rows
        query_cot, key_cot, value_cot = attend_backward(
            query_block,
            key_window,
            value_window,
            allowed,
            log_totals[block_index],
            out_grad,
            attention,
            group_size,
        )
        query_acc = query_cot
        region = pair_acc + jnp.stack([key_cot, value_cot])
        pair_acc = region
        return (query_acc, pair_acc)

    query_zero = jnp.zeros((token_count, query_weight.shape[1]), jnp.float32)
    pair_zero = jnp.zeros((2, (reach_blocks + 1) * token_count, key_weight.shape[1]), jnp.float32)
    query_acc, pair_acc = lax.fori_loop(0, block_count, backward_block, (query_zero, pair_zero))
    grad_query = query_back(query_acc)[0].astype(jnp.bfloat16)
    grad_scale = float(lax.axis_size("ctx") * token_count) ** (-0.5)
    contract = (((0,), (0,)), ((), ()))
    own_pair = pair_acc[:, reach_blocks * token_count :]
    for distance in range(1, reach_blocks + 1):
        lower_row = (reach_blocks - distance) * token_count
        own_pair = own_pair + passed_along(
            pair_acc[:, lower_row : lower_row + token_count], "ctx", -distance
        )
    grad_key = key_back(own_pair[0])[0].astype(jnp.bfloat16)
    grad_value = own_pair[1].astype(jnp.bfloat16)
    grad_cat = jnp.concatenate([grad_query, grad_key, grad_value], axis=1)
    summed = ctx_scatter_sum(
        (
            lax.dot_general(gathered, grad_cat, contract, preferred_element_type=jnp.float32)
            * grad_scale
        ).astype(jnp.bfloat16),
        "ctx",
        (lax.axis_size("ctx") // 4, 2, 2),
    )
    query_weight_grad = summed[:, :query_width]
    key_weight_grad = summed[:, query_width : query_width + key_width]
    value_weight_grad = summed[:, query_width + key_width :]
    back_contract = (((1,), (1,)), ((), ()))
    input_grad = exchange_sum(
        lax.dot_general(
            grad_cat, weight_cat, back_contract, preferred_element_type=jnp.float32
        ).astype(jnp.bfloat16),
        "heads",
    ).astype(jnp.bfloat16)
    return (attention, input_grad, query_weight_grad, key_weight_grad, value_weight_grad)


def solution(mesh):
    return jax.shard_map(
        per_device,
        mesh=mesh,
        in_specs=(
            P(("ctx", "heads"), None),
            P(None, "heads"),
            P(None, "heads"),
            P(None, "heads"),
            P(),
            P(),
            P("ctx", "heads"),
        ),
        out_specs=(
            P("ctx", "heads"),
            P(("ctx", "heads"), None),
            P("ctx", "heads"),
            P("ctx", "heads"),
            P("ctx", "heads"),
        ),
        check_vma=False,
    )
```

```python
import math

import jax
import jax.numpy as jnp
from jax import lax
from jax.sharding import PartitionSpec as P

HEAD_DIM = 128
WINDOW = 1024
SCALAR = 168
HEADS = 16
KV_HEADS = 8


def passed_along(block, axis, distance):
    devices = range(lax.axis_size(axis))
    route = [(i - distance, i) for i in devices if i - distance in devices]
    return lax.ppermute(block, axis, route)


def torus_shifts(axis):
    size = lax.axis_size(axis)
    inner = size // 2 if size >= 4 else size
    outer = size // inner
    me = lax.axis_index(axis)

    def moved(index, dx, dy):
        return ((index // inner + dx) % outer) * inner + (index % inner + dy) % inner

    shifts = [(dx, dy) for dx in range(outer) for dy in range(inner)][1:]
    routes = [[(i, moved(i, dx, dy)) for i in range(size)] for dx, dy in shifts]
    targets = [moved(me, dx, dy) for dx, dy in shifts]
    slot_of = [
        ((me // inner - j // inner) % outer) * inner + (me % inner - j % inner) % inner
        for j in range(size)
    ]
    return (size, me, routes, targets, slot_of)


def gather_over(block, axis):
    size, me, routes, targets, slot_of = torus_shifts(axis)
    slots = jnp.stack([block] + [lax.ppermute(block, axis, route) for route in routes])
    order = jnp.stack([jnp.asarray(s, jnp.int32) for s in slot_of])
    return jnp.take(slots, order, axis=0).reshape((size * block.shape[0],) + block.shape[1:])


def scatter_sum_over(full, axis):
    size, me, routes, targets, slot_of = torus_shifts(axis)
    pieces = full.reshape((size, full.shape[0] // size) + full.shape[1:])
    total = lax.dynamic_index_in_dim(pieces, me, 0, keepdims=False).astype(jnp.float32)
    for route, target in zip(routes, targets):
        piece = lax.dynamic_index_in_dim(pieces, target, 0, keepdims=False)
        total = total + lax.ppermute(piece, axis, route).astype(jnp.float32)
    return total


def ring_scatter_sum(blocks, axis, count, stride):
    size = lax.axis_size(axis)
    me = lax.axis_index(axis)
    digit = (me // stride) % count
    half = blocks.shape[-1] // 2

    def route(step):
        return [
            (i, i - ((i // stride) % count) * stride + (((i // stride) % count + step) % count) * stride)
            for i in range(size)
        ]

    def chunk(k, step, lo):
        block = lax.dynamic_index_in_dim(blocks, (digit - step * (k + 1)) % count, 0, keepdims=False)
        return block[..., lo : lo + half]

    def advance(k, carry):
        up, down = carry
        up = lax.ppermute(up.astype(jnp.bfloat16), axis, route(1)).astype(jnp.float32)
        down = lax.ppermute(down.astype(jnp.bfloat16), axis, route(-1)).astype(jnp.float32)
        return (up + chunk(k + 1, 1, 0), down + chunk(k + 1, -1, half))

    up, down = lax.fori_loop(0, count - 1, advance, (chunk(0, 1, 0), chunk(0, -1, half)))
    return jnp.concatenate([up, down], axis=-1)


def pair_scatter_sum(blocks, axis, stride):
    size = lax.axis_size(axis)
    me = lax.axis_index(axis)
    digit = (me // stride) % 2
    route = [(i, i + stride if (i // stride) % 2 == 0 else i - stride) for i in range(size)]
    own = lax.dynamic_index_in_dim(blocks, digit, 0, keepdims=False).astype(jnp.float32)
    other = lax.dynamic_index_in_dim(blocks, 1 - digit, 0, keepdims=False)
    return own + lax.ppermute(other.astype(jnp.bfloat16), axis, route).astype(jnp.float32)


def ctx_scatter_sum(full, axis, levels):
    outer, middle, inner = levels
    width = full.shape[1]
    grid = full.reshape(outer, middle, inner, -1, width)
    grid = jnp.moveaxis(grid, 2, 0)
    grid = pair_scatter_sum(grid, axis, 1)
    grid = ring_scatter_sum(grid, axis, outer, middle * inner)
    return pair_scatter_sum(grid, axis, inner)


def gather_all(block, axis):
    size = lax.axis_size(axis)
    copies = jnp.broadcast_to(block[None], (size,) + block.shape)
    received = lax.all_to_all(copies, axis, 0, 0)
    return received.reshape((size * block.shape[0],) + block.shape[1:])


def exchange_sum(full, axis):
    size = lax.axis_size(axis)
    pieces = full.reshape((size, full.shape[0] // size) + full.shape[1:])
    received = lax.all_to_all(pieces, axis, 0, 0)
    return jnp.sum(received.astype(jnp.float32), axis=0)


def rope_tables(positions, head_size):
    half_size = head_size // 2
    indices = jnp.arange(half_size, dtype=jnp.float32)
    inverse = jnp.exp(indices * (-2.0 * math.log(10000.0) / head_size))
    angles = positions.astype(jnp.float32)[:, None] * inverse[None, :]
    return (jnp.cos(angles), jnp.sin(angles))


def prepare(projected, cosine, sine_table, channel_gain, factor):
    row_count = projected.shape[0]
    head_size = channel_gain.shape[0]
    pieces = projected.reshape(row_count, -1, head_size)
    normed = (
        pieces * lax.rsqrt(jnp.mean(pieces * pieces, axis=-1, keepdims=True) + 1e-06) * channel_gain
    )
    half_size = head_size // 2
    leading = normed[..., :half_size]
    trailing = normed[..., half_size:]
    cos_rows = cosine[:, None, :]
    sin_rows = sine_table[:, None, :]
    turned = jnp.concatenate(
        [leading * cos_rows - trailing * sin_rows, trailing * cos_rows + leading * sin_rows],
        axis=-1,
    )
    return (turned * factor).reshape(row_count, -1)


def band_mask(query_pos, key_pos):
    separation = query_pos[:, None] - key_pos[None, :]
    return (separation >= 0) & (separation < WINDOW) & (key_pos[None, :] >= 0)


def head_grids(query_block, key_window, value_window, group_size):
    query_grid = query_block.reshape(query_block.shape[0], -1, group_size, HEAD_DIM)
    key_grid = key_window.reshape(key_window.shape[0], -1, HEAD_DIM)
    value_grid = value_window.reshape(value_window.shape[0], -1, HEAD_DIM)
    return (query_grid, key_grid, value_grid)


def attend_forward(query_block, key_window, value_window, allowed, group_size):
    query_grid, key_grid, value_grid = head_grids(query_block, key_window, value_window, group_size)
    scores = jnp.einsum("qkgd,jkd->kgqj", query_grid, key_grid, preferred_element_type=jnp.float32)
    masked = jnp.where(allowed, scores, -1e30)
    highest = jnp.max(masked, axis=-1, keepdims=True)
    total = jnp.sum(jnp.exp(masked - highest), axis=-1, keepdims=True)
    log_total = highest + jnp.log(total)
    weights = jnp.where(allowed, jnp.exp(masked - log_total), 0.0)
    output = jnp.einsum(
        "kgqj,jkd->qkgd",
        weights.astype(jnp.bfloat16),
        value_grid,
        preferred_element_type=jnp.float32,
    )
    return (output.reshape(query_block.shape[0], -1), log_total[..., 0])


def attend_backward(
    query_block,
    key_window,
    value_window,
    allowed,
    log_total,
    out_block,
    attention_block,
    group_size,
):
    query_grid, key_grid, value_grid = head_grids(query_block, key_window, value_window, group_size)
    row_count = query_block.shape[0]
    grad_grid = out_block.reshape(row_count, -1, group_size, HEAD_DIM)
    attention_grid = attention_block.reshape(row_count, -1, group_size, HEAD_DIM)
    scores = jnp.einsum("qkgd,jkd->kgqj", query_grid, key_grid, preferred_element_type=jnp.float32)
    masked = jnp.where(allowed, scores, -1e30)
    weights = jnp.where(allowed, jnp.exp(masked - log_total[..., None]), 0.0)
    delta = jnp.einsum(
        "qkgd,qkgd->kgq", grad_grid, attention_grid, preferred_element_type=jnp.float32
    )
    products = jnp.einsum(
        "qkgd,jkd->kgqj", grad_grid, value_grid, preferred_element_type=jnp.float32
    )
    shifts = (weights * (products - delta[..., None])).astype(jnp.bfloat16)
    query_cot = jnp.einsum(
        "kgqj,jkd->qkgd", shifts, key_grid, preferred_element_type=jnp.float32
    ).reshape(row_count, -1)
    key_cot = jnp.einsum(
        "kgqj,qkgd->jkd", shifts, query_grid, preferred_element_type=jnp.float32
    ).reshape(key_window.shape[0], -1)
    value_cot = jnp.einsum(
        "kgqj,qkgd->jkd",
        weights.astype(jnp.bfloat16),
        grad_grid,
        preferred_element_type=jnp.float32,
    ).reshape(key_window.shape[0], -1)
    return (query_cot, key_cot, value_cot)


def per_device(hidden, query_weight, key_weight, value_weight, query_gain, key_gain, out_grad):
    token_count = out_grad.shape[0]
    group_size = HEADS // KV_HEADS
    block_rows = min(token_count, 512)
    block_count = token_count // block_rows
    window_rows = block_rows + WINDOW
    reach_blocks = (WINDOW - 2) // token_count + 1
    position_base = lax.axis_index("ctx") * token_count
    gathered = gather_all(hidden, "heads")
    query_width = query_weight.shape[1]
    key_width = key_weight.shape[1]
    weight_cat = jnp.concatenate([query_weight, key_weight, value_weight], axis=1)
    projected = jnp.dot(gathered, weight_cat, preferred_element_type=jnp.float32)
    query_proj = projected[:, :query_width]
    key_proj = projected[:, query_width : query_width + key_width]
    value_proj = projected[:, query_width + key_width :]
    positions = position_base + jnp.arange(token_count, dtype=jnp.int32)
    cosine, sine_table = rope_tables(positions, HEAD_DIM)
    query_full, query_back = jax.vjp(
        lambda projected: prepare(projected, cosine, sine_table, query_gain, SCALAR ** (-0.5)),
        query_proj,
    )
    key_full, key_back = jax.vjp(
        lambda projected: prepare(projected, cosine, sine_table, key_gain, 1.0), key_proj
    )
    query_cast = query_full.astype(jnp.bfloat16)
    key_value = jnp.stack([key_full.astype(jnp.bfloat16), value_proj.astype(jnp.bfloat16)])
    received = [passed_along(key_value, "ctx", distance) for distance in range(1, reach_blocks + 1)]
    window_pair = jnp.concatenate(received[::-1] + [key_value], axis=1)
    key_span = window_pair[0]
    value_span = window_pair[1]

    def window_of(block_index):
        block_start = block_index * block_rows
        query_pos = position_base + block_start + jnp.arange(block_rows, dtype=jnp.int32)
        key_pos = position_base - WINDOW + block_start + jnp.arange(window_rows, dtype=jnp.int32)
        return (query_cast, key_span, value_span, band_mask(query_pos, key_pos))

    def forward_block(block_index):
        query_block, key_window, value_window, allowed = window_of(block_index)
        return attend_forward(query_block, key_window, value_window, allowed, group_size)

    outputs, log_totals = lax.map(forward_block, jnp.arange(block_count, dtype=jnp.int32))
    attention = outputs.reshape(token_count, -1).astype(jnp.bfloat16)

    def backward_block(block_index, carry):
        query_acc, pair_acc = carry
        query_block, key_window, value_window, allowed = window_of(block_index)
        block_start = block_index * block_rows
        query_cot, key_cot, value_cot = attend_backward(
            query_block,
            key_window,
            value_window,
            allowed,
            log_totals[block_index],
            out_grad,
            attention,
            group_size,
        )
        query_acc = query_cot
        region = pair_acc + jnp.stack([key_cot, value_cot])
        pair_acc = region
        return (query_acc, pair_acc)

    query_zero = jnp.zeros((token_count, query_weight.shape[1]), jnp.float32)
    pair_zero = jnp.zeros((2, (reach_blocks + 1) * token_count, key_weight.shape[1]), jnp.float32)
    query_acc, pair_acc = lax.fori_loop(0, block_count, backward_block, (query_zero, pair_zero))
    grad_query = query_back(query_acc)[0].astype(jnp.bfloat16)
    grad_scale = float(lax.axis_size("ctx") * token_count) ** (-0.5)
    contract = (((0,), (0,)), ((), ()))
    own_pair = pair_acc[:, reach_blocks * token_count :]
    for distance in range(1, reach_blocks + 1):
        lower_row = (reach_blocks - distance) * token_count
        own_pair = own_pair + passed_along(
            pair_acc[:, lower_row : lower_row + token_count].astype(jnp.bfloat16), "ctx", -distance
        ).astype(jnp.float32)
    grad_key = key_back(own_pair[0])[0].astype(jnp.bfloat16)
    grad_value = own_pair[1].astype(jnp.bfloat16)
    grad_cat = jnp.concatenate([grad_query, grad_key, grad_value], axis=1)
    summed = ctx_scatter_sum(
        (
            lax.dot_general(gathered, grad_cat, contract, preferred_element_type=jnp.float32)
            * grad_scale
        ).astype(jnp.bfloat16),
        "ctx",
        (lax.axis_size("ctx") // 4, 2, 2),
    )
    query_weight_grad = summed[:, :query_width]
    key_weight_grad = summed[:, query_width : query_width + key_width]
    value_weight_grad = summed[:, query_width + key_width :]
    back_contract = (((1,), (1,)), ((), ()))
    input_grad = exchange_sum(
        lax.dot_general(
            grad_cat, weight_cat, back_contract, preferred_element_type=jnp.float32
        ).astype(jnp.bfloat16),
        "heads",
    ).astype(jnp.bfloat16)
    return (attention, input_grad, query_weight_grad, key_weight_grad, value_weight_grad)


def solution(mesh):
    return jax.shard_map(
        per_device,
        mesh=mesh,
        in_specs=(
            P(("ctx", "heads"), None),
            P(None, "heads"),
            P(None, "heads"),
            P(None, "heads"),
            P(),
            P(),
            P("ctx", "heads"),
        ),
        out_specs=(
            P("ctx", "heads"),
            P(("ctx", "heads"), None),
            P("ctx", "heads"),
            P("ctx", "heads"),
            P("ctx", "heads"),
        ),
        check_vma=False,
    )
```

```python
import math

import jax
import jax.numpy as jnp
from jax import lax
from jax.sharding import PartitionSpec as P

HEAD_DIM = 128
WINDOW = 1024
SCALAR = 168
HEADS = 16
KV_HEADS = 8


def passed_along(block, axis, distance):
    devices = range(lax.axis_size(axis))
    route = [(i - distance, i) for i in devices if i - distance in devices]
    return lax.ppermute(block, axis, route)


def torus_shifts(axis):
    size = lax.axis_size(axis)
    inner = size // 2 if size >= 4 else size
    outer = size // inner
    me = lax.axis_index(axis)

    def moved(index, dx, dy):
        return ((index // inner + dx) % outer) * inner + (index % inner + dy) % inner

    shifts = [(dx, dy) for dx in range(outer) for dy in range(inner)][1:]
    routes = [[(i, moved(i, dx, dy)) for i in range(size)] for dx, dy in shifts]
    targets = [moved(me, dx, dy) for dx, dy in shifts]
    slot_of = [
        ((me // inner - j // inner) % outer) * inner + (me % inner - j % inner) % inner
        for j in range(size)
    ]
    return (size, me, routes, targets, slot_of)


def gather_over(block, axis):
    size, me, routes, targets, slot_of = torus_shifts(axis)
    slots = jnp.stack([block] + [lax.ppermute(block, axis, route) for route in routes])
    order = jnp.stack([jnp.asarray(s, jnp.int32) for s in slot_of])
    return jnp.take(slots, order, axis=0).reshape((size * block.shape[0],) + block.shape[1:])


def scatter_sum_over(full, axis):
    size, me, routes, targets, slot_of = torus_shifts(axis)
    pieces = full.reshape((size, full.shape[0] // size) + full.shape[1:])
    total = lax.dynamic_index_in_dim(pieces, me, 0, keepdims=False).astype(jnp.float32)
    for route, target in zip(routes, targets):
        piece = lax.dynamic_index_in_dim(pieces, target, 0, keepdims=False)
        total = total + lax.ppermute(piece, axis, route).astype(jnp.float32)
    return total


def ring_scatter_sum(blocks, axis, count, stride):
    size = lax.axis_size(axis)
    me = lax.axis_index(axis)
    digit = (me // stride) % count
    half = blocks.shape[-1] // 2

    def route(step):
        return [
            (i, i - ((i // stride) % count) * stride + (((i // stride) % count + step) % count) * stride)
            for i in range(size)
        ]

    def chunk(k, step, lo):
        block = lax.dynamic_index_in_dim(blocks, (digit - step * (k + 1)) % count, 0, keepdims=False)
        return block[..., lo : lo + half]

    def advance(k, carry):
        up, down = carry
        up = lax.ppermute(up.astype(jnp.bfloat16), axis, route(1)).astype(jnp.float32)
        down = lax.ppermute(down.astype(jnp.bfloat16), axis, route(-1)).astype(jnp.float32)
        return (up + chunk(k + 1, 1, 0), down + chunk(k + 1, -1, half))

    up, down = lax.fori_loop(0, count - 1, advance, (chunk(0, 1, 0), chunk(0, -1, half)))
    return jnp.concatenate([up, down], axis=-1)


def pair_scatter_sum(blocks, axis, stride):
    size = lax.axis_size(axis)
    me = lax.axis_index(axis)
    digit = (me // stride) % 2
    route = [(i, i + stride if (i // stride) % 2 == 0 else i - stride) for i in range(size)]
    own = lax.dynamic_index_in_dim(blocks, digit, 0, keepdims=False).astype(jnp.float32)
    other = lax.dynamic_index_in_dim(blocks, 1 - digit, 0, keepdims=False)
    return own + lax.ppermute(other.astype(jnp.bfloat16), axis, route).astype(jnp.float32)


def ctx_scatter_sum(full, axis, levels):
    outer, middle, inner = levels
    width = full.shape[1]
    grid = full.reshape(outer, middle, inner, -1, width)
    grid = jnp.moveaxis(grid, 2, 0)
    grid = pair_scatter_sum(grid, axis, 1)
    grid = ring_scatter_sum(grid, axis, outer, middle * inner)
    return pair_scatter_sum(grid, axis, inner)


def gather_all(block, axis):
    size = lax.axis_size(axis)
    copies = jnp.broadcast_to(block[None], (size,) + block.shape)
    received = lax.all_to_all(copies, axis, 0, 0)
    return received.reshape((size * block.shape[0],) + block.shape[1:])


def exchange_sum(full, axis):
    size = lax.axis_size(axis)
    pieces = full.reshape((size, full.shape[0] // size) + full.shape[1:])
    received = lax.all_to_all(pieces, axis, 0, 0)
    return jnp.sum(received.astype(jnp.float32), axis=0)


def rope_tables(positions, head_size):
    half_size = head_size // 2
    indices = jnp.arange(half_size, dtype=jnp.float32)
    inverse = jnp.exp(indices * (-2.0 * math.log(10000.0) / head_size))
    angles = positions.astype(jnp.float32)[:, None] * inverse[None, :]
    return (jnp.cos(angles), jnp.sin(angles))


def prepare(projected, cosine, sine_table, channel_gain, factor):
    row_count = projected.shape[0]
    head_size = channel_gain.shape[0]
    pieces = projected.reshape(row_count, -1, head_size)
    normed = (
        pieces * lax.rsqrt(jnp.mean(pieces * pieces, axis=-1, keepdims=True) + 1e-06) * channel_gain
    )
    half_size = head_size // 2
    leading = normed[..., :half_size]
    trailing = normed[..., half_size:]
    cos_rows = cosine[:, None, :]
    sin_rows = sine_table[:, None, :]
    turned = jnp.concatenate(
        [leading * cos_rows - trailing * sin_rows, trailing * cos_rows + leading * sin_rows],
        axis=-1,
    )
    return (turned * factor).reshape(row_count, -1)


def band_mask(query_pos, key_pos):
    separation = query_pos[:, None] - key_pos[None, :]
    return (separation >= 0) & (separation < WINDOW) & (key_pos[None, :] >= 0)


def head_grids(query_block, key_window, value_window, group_size):
    query_grid = query_block.reshape(query_block.shape[0], -1, group_size, HEAD_DIM)
    key_grid = key_window.reshape(key_window.shape[0], -1, HEAD_DIM)
    value_grid = value_window.reshape(value_window.shape[0], -1, HEAD_DIM)
    return (query_grid, key_grid, value_grid)


def attend_forward(query_block, key_window, value_window, allowed, group_size):
    query_grid, key_grid, value_grid = head_grids(query_block, key_window, value_window, group_size)
    scores = jnp.einsum("qkgd,jkd->kgqj", query_grid, key_grid, preferred_element_type=jnp.float32)
    masked = jnp.where(allowed, scores, -1e30)
    highest = jnp.max(masked, axis=-1, keepdims=True)
    total = jnp.sum(jnp.exp(masked - highest), axis=-1, keepdims=True)
    log_total = highest + jnp.log(total)
    weights = jnp.where(allowed, jnp.exp(masked - log_total), 0.0)
    output = jnp.einsum(
        "kgqj,jkd->qkgd",
        weights.astype(jnp.bfloat16),
        value_grid,
        preferred_element_type=jnp.float32,
    )
    return (output.reshape(query_block.shape[0], -1), log_total[..., 0])


def attend_backward(
    query_block,
    key_window,
    value_window,
    allowed,
    log_total,
    out_block,
    attention_block,
    group_size,
):
    query_grid, key_grid, value_grid = head_grids(query_block, key_window, value_window, group_size)
    row_count = query_block.shape[0]
    grad_grid = out_block.reshape(row_count, -1, group_size, HEAD_DIM)
    attention_grid = attention_block.reshape(row_count, -1, group_size, HEAD_DIM)
    scores = jnp.einsum("qkgd,jkd->kgqj", query_grid, key_grid, preferred_element_type=jnp.float32)
    masked = jnp.where(allowed, scores, -1e30)
    weights = jnp.where(allowed, jnp.exp(masked - log_total[..., None]), 0.0)
    delta = jnp.einsum(
        "qkgd,qkgd->kgq", grad_grid, attention_grid, preferred_element_type=jnp.float32
    )
    products = jnp.einsum(
        "qkgd,jkd->kgqj", grad_grid, value_grid, preferred_element_type=jnp.float32
    )
    shifts = (weights * (products - delta[..., None])).astype(jnp.bfloat16)
    query_cot = jnp.einsum(
        "kgqj,jkd->qkgd", shifts, key_grid, preferred_element_type=jnp.float32
    ).reshape(row_count, -1)
    key_cot = jnp.einsum(
        "kgqj,qkgd->jkd", shifts, query_grid, preferred_element_type=jnp.float32
    ).reshape(key_window.shape[0], -1)
    value_cot = jnp.einsum(
        "kgqj,qkgd->jkd",
        weights.astype(jnp.bfloat16),
        grad_grid,
        preferred_element_type=jnp.float32,
    ).reshape(key_window.shape[0], -1)
    return (query_cot, key_cot, value_cot)


def per_device(hidden, query_weight, key_weight, value_weight, query_gain, key_gain, out_grad):
    token_count = out_grad.shape[0]
    group_size = HEADS // KV_HEADS
    block_rows = min(token_count, 512)
    block_count = token_count // block_rows
    window_rows = block_rows + WINDOW
    reach_blocks = (WINDOW - 2) // token_count + 1
    position_base = lax.axis_index("ctx") * token_count
    gathered = gather_all(hidden, "heads")
    query_width = query_weight.shape[1]
    key_width = key_weight.shape[1]
    weight_cat = jnp.concatenate([query_weight, key_weight, value_weight], axis=1)
    projected = jnp.dot(gathered, weight_cat, preferred_element_type=jnp.float32)
    query_proj = projected[:, :query_width]
    key_proj = projected[:, query_width : query_width + key_width]
    value_proj = projected[:, query_width + key_width :]
    positions = position_base + jnp.arange(token_count, dtype=jnp.int32)
    cosine, sine_table = rope_tables(positions, HEAD_DIM)
    query_full, query_back = jax.vjp(
        lambda projected: prepare(projected, cosine, sine_table, query_gain, SCALAR ** (-0.5)),
        query_proj,
    )
    key_full, key_back = jax.vjp(
        lambda projected: prepare(projected, cosine, sine_table, key_gain, 1.0), key_proj
    )
    query_cast = query_full.astype(jnp.bfloat16)
    key_value = jnp.stack([key_full.astype(jnp.bfloat16), value_proj.astype(jnp.bfloat16)])
    received = [passed_along(key_value, "ctx", distance) for distance in range(1, reach_blocks + 1)]
    window_pair = jnp.concatenate(received[::-1] + [key_value], axis=1)
    key_span = window_pair[0]
    value_span = window_pair[1]

    def window_of(block_index):
        block_start = block_index * block_rows
        query_pos = position_base + block_start + jnp.arange(block_rows, dtype=jnp.int32)
        key_pos = position_base - WINDOW + block_start + jnp.arange(window_rows, dtype=jnp.int32)
        return (query_cast, key_span, value_span, band_mask(query_pos, key_pos))

    def forward_block(block_index):
        query_block, key_window, value_window, allowed = window_of(block_index)
        return attend_forward(query_block, key_window, value_window, allowed, group_size)

    outputs, log_totals = lax.map(forward_block, jnp.arange(block_count, dtype=jnp.int32))
    attention = outputs.reshape(token_count, -1).astype(jnp.bfloat16)

    def backward_block(block_index, carry):
        query_acc, pair_acc = carry
        query_block, key_window, value_window, allowed = window_of(block_index)
        block_start = block_index * block_rows
        query_cot, key_cot, value_cot = attend_backward(
            query_block,
            key_window,
            value_window,
            allowed,
            log_totals[block_index],
            out_grad,
            attention,
            group_size,
        )
        query_acc = query_cot
        region = pair_acc + jnp.stack([key_cot, value_cot])
        pair_acc = region
        return (query_acc, pair_acc)

    query_zero = jnp.zeros((token_count, query_weight.shape[1]), jnp.float32)
    pair_zero = jnp.zeros((2, (reach_blocks + 1) * token_count, key_weight.shape[1]), jnp.float32)
    query_acc, pair_acc = lax.fori_loop(0, block_count, backward_block, (query_zero, pair_zero))
    grad_query = query_back(query_acc)[0].astype(jnp.bfloat16)
    grad_scale = float(lax.axis_size("ctx") * token_count) ** (-0.5)
    contract = (((0,), (0,)), ((), ()))
    own_pair = pair_acc[:, reach_blocks * token_count :]
    for distance in range(1, reach_blocks + 1):
        lower_row = (reach_blocks - distance) * token_count
        own_pair = own_pair + passed_along(
            pair_acc[:, lower_row : lower_row + token_count].astype(jnp.bfloat16), "ctx", -distance
        ).astype(jnp.float32)
    grad_key = key_back(own_pair[0])[0].astype(jnp.bfloat16)
    grad_value = own_pair[1].astype(jnp.bfloat16)
    grad_cat = jnp.concatenate([grad_query, grad_key, grad_value], axis=1)
    back_contract = (((1,), (1,)), ((), ()))
    input_partial = lax.dot_general(
        grad_cat, weight_cat, back_contract, preferred_element_type=jnp.float32
    ).astype(jnp.bfloat16)
    input_partial, hidden_late = lax.optimization_barrier((input_partial, gathered))
    input_grad = exchange_sum(input_partial, "heads").astype(jnp.bfloat16)
    summed = ctx_scatter_sum(
        (
            lax.dot_general(hidden_late, grad_cat, contract, preferred_element_type=jnp.float32)
            * grad_scale
        ).astype(jnp.bfloat16),
        "ctx",
        (lax.axis_size("ctx") // 4, 2, 2),
    )
    query_weight_grad = summed[:, :query_width]
    key_weight_grad = summed[:, query_width : query_width + key_width]
    value_weight_grad = summed[:, query_width + key_width :]
    return (attention, input_grad, query_weight_grad, key_weight_grad, value_weight_grad)


def solution(mesh):
    return jax.shard_map(
        per_device,
        mesh=mesh,
        in_specs=(
            P(("ctx", "heads"), None),
            P(None, "heads"),
            P(None, "heads"),
            P(None, "heads"),
            P(),
            P(),
            P("ctx", "heads"),
        ),
        out_specs=(
            P("ctx", "heads"),
            P(("ctx", "heads"), None),
            P("ctx", "heads"),
            P("ctx", "heads"),
            P("ctx", "heads"),
        ),
        check_vma=False,
    )
```

```python
import math

import jax
import jax.numpy as jnp
from jax import lax
from jax.sharding import PartitionSpec as P

HEAD_DIM = 128
WINDOW = 1024
SCALAR = 168
HEADS = 16
KV_HEADS = 8


def passed_along(block, axis, distance):
    devices = range(lax.axis_size(axis))
    route = [(i - distance, i) for i in devices if i - distance in devices]
    return lax.ppermute(block, axis, route)


def torus_shifts(axis):
    size = lax.axis_size(axis)
    inner = size // 2 if size >= 4 else size
    outer = size // inner
    me = lax.axis_index(axis)

    def moved(index, dx, dy):
        return ((index // inner + dx) % outer) * inner + (index % inner + dy) % inner

    shifts = [(dx, dy) for dx in range(outer) for dy in range(inner)][1:]
    routes = [[(i, moved(i, dx, dy)) for i in range(size)] for dx, dy in shifts]
    targets = [moved(me, dx, dy) for dx, dy in shifts]
    slot_of = [
        ((me // inner - j // inner) % outer) * inner + (me % inner - j % inner) % inner
        for j in range(size)
    ]
    return (size, me, routes, targets, slot_of)


def gather_over(block, axis):
    size, me, routes, targets, slot_of = torus_shifts(axis)
    slots = jnp.stack([block] + [lax.ppermute(block, axis, route) for route in routes])
    order = jnp.stack([jnp.asarray(s, jnp.int32) for s in slot_of])
    return jnp.take(slots, order, axis=0).reshape((size * block.shape[0],) + block.shape[1:])


def scatter_sum_over(full, axis):
    size, me, routes, targets, slot_of = torus_shifts(axis)
    pieces = full.reshape((size, full.shape[0] // size) + full.shape[1:])
    total = lax.dynamic_index_in_dim(pieces, me, 0, keepdims=False).astype(jnp.float32)
    for route, target in zip(routes, targets):
        piece = lax.dynamic_index_in_dim(pieces, target, 0, keepdims=False)
        total = total + lax.ppermute(piece, axis, route).astype(jnp.float32)
    return total


def ring_scatter_sum(blocks, axis, count, stride, lane_stride):
    size = lax.axis_size(axis)
    me = lax.axis_index(axis)
    digit = (me // stride) % count
    step = 1 - 2 * ((me // lane_stride) % 2)

    def target(i):
        place = (i // stride) % count
        turn = 1 - 2 * ((i // lane_stride) % 2)
        return i + ((place + turn) % count - place) * stride

    route = [(i, target(i)) for i in range(size)]

    def chunk(k):
        return lax.dynamic_index_in_dim(blocks, (digit - step * (k + 1)) % count, 0, keepdims=False)

    def advance(k, running):
        received = lax.ppermute(running.astype(jnp.bfloat16), axis, route).astype(jnp.float32)
        return received + chunk(k + 1)

    return lax.fori_loop(0, count - 1, advance, chunk(0))


def pair_scatter_sum(blocks, axis, stride):
    size = lax.axis_size(axis)
    me = lax.axis_index(axis)
    digit = (me // stride) % 2
    route = [(i, i + stride if (i // stride) % 2 == 0 else i - stride) for i in range(size)]
    own = lax.dynamic_index_in_dim(blocks, digit, 0, keepdims=False).astype(jnp.float32)
    other = lax.dynamic_index_in_dim(blocks, 1 - digit, 0, keepdims=False)
    return own + lax.ppermute(other.astype(jnp.bfloat16), axis, route).astype(jnp.float32)


def ctx_scatter_sum(full, axis, levels):
    outer, middle, inner = levels
    width = full.shape[1]
    grid = full.reshape(outer, middle, inner, -1, width)
    grid = jnp.moveaxis(grid, 2, 0)
    grid = pair_scatter_sum(grid, axis, 1)
    grid = ring_scatter_sum(grid, axis, outer, middle * inner, 1)
    return pair_scatter_sum(grid, axis, inner)


def gather_all(block, axis):
    size = lax.axis_size(axis)
    copies = jnp.broadcast_to(block[None], (size,) + block.shape)
    received = lax.all_to_all(copies, axis, 0, 0)
    return received.reshape((size * block.shape[0],) + block.shape[1:])


def exchange_sum(full, axis):
    size = lax.axis_size(axis)
    pieces = full.reshape((size, full.shape[0] // size) + full.shape[1:])
    received = lax.all_to_all(pieces, axis, 0, 0)
    return jnp.sum(received.astype(jnp.float32), axis=0)


def rope_tables(positions, head_size):
    half_size = head_size // 2
    indices = jnp.arange(half_size, dtype=jnp.float32)
    inverse = jnp.exp(indices * (-2.0 * math.log(10000.0) / head_size))
    angles = positions.astype(jnp.float32)[:, None] * inverse[None, :]
    return (jnp.cos(angles), jnp.sin(angles))


def prepare(projected, cosine, sine_table, channel_gain, factor):
    row_count = projected.shape[0]
    head_size = channel_gain.shape[0]
    pieces = projected.reshape(row_count, -1, head_size)
    normed = (
        pieces * lax.rsqrt(jnp.mean(pieces * pieces, axis=-1, keepdims=True) + 1e-06) * channel_gain
    )
    half_size = head_size // 2
    leading = normed[..., :half_size]
    trailing = normed[..., half_size:]
    cos_rows = cosine[:, None, :]
    sin_rows = sine_table[:, None, :]
    turned = jnp.concatenate(
        [leading * cos_rows - trailing * sin_rows, trailing * cos_rows + leading * sin_rows],
        axis=-1,
    )
    return (turned * factor).reshape(row_count, -1)


def band_mask(query_pos, key_pos):
    separation = query_pos[:, None] - key_pos[None, :]
    return (separation >= 0) & (separation < WINDOW) & (key_pos[None, :] >= 0)


def head_grids(query_block, key_window, value_window, group_size):
    query_grid = query_block.reshape(query_block.shape[0], -1, group_size, HEAD_DIM)
    key_grid = key_window.reshape(key_window.shape[0], -1, HEAD_DIM)
    value_grid = value_window.reshape(value_window.shape[0], -1, HEAD_DIM)
    return (query_grid, key_grid, value_grid)


def attend_forward(query_block, key_window, value_window, allowed, group_size):
    query_grid, key_grid, value_grid = head_grids(query_block, key_window, value_window, group_size)
    scores = jnp.einsum("qkgd,jkd->kgqj", query_grid, key_grid, preferred_element_type=jnp.float32)
    masked = jnp.where(allowed, scores, -1e30)
    highest = jnp.max(masked, axis=-1, keepdims=True)
    total = jnp.sum(jnp.exp(masked - highest), axis=-1, keepdims=True)
    log_total = highest + jnp.log(total)
    weights = jnp.where(allowed, jnp.exp(masked - log_total), 0.0)
    output = jnp.einsum(
        "kgqj,jkd->qkgd",
        weights.astype(jnp.bfloat16),
        value_grid,
        preferred_element_type=jnp.float32,
    )
    return (output.reshape(query_block.shape[0], -1), log_total[..., 0])


def attend_backward(
    query_block,
    key_window,
    value_window,
    allowed,
    log_total,
    out_block,
    attention_block,
    group_size,
):
    query_grid, key_grid, value_grid = head_grids(query_block, key_window, value_window, group_size)
    row_count = query_block.shape[0]
    grad_grid = out_block.reshape(row_count, -1, group_size, HEAD_DIM)
    attention_grid = attention_block.reshape(row_count, -1, group_size, HEAD_DIM)
    scores = jnp.einsum("qkgd,jkd->kgqj", query_grid, key_grid, preferred_element_type=jnp.float32)
    masked = jnp.where(allowed, scores, -1e30)
    weights = jnp.where(allowed, jnp.exp(masked - log_total[..., None]), 0.0)
    delta = jnp.einsum(
        "qkgd,qkgd->kgq", grad_grid, attention_grid, preferred_element_type=jnp.float32
    )
    products = jnp.einsum(
        "qkgd,jkd->kgqj", grad_grid, value_grid, preferred_element_type=jnp.float32
    )
    shifts = (weights * (products - delta[..., None])).astype(jnp.bfloat16)
    query_cot = jnp.einsum(
        "kgqj,jkd->qkgd", shifts, key_grid, preferred_element_type=jnp.float32
    ).reshape(row_count, -1)
    key_cot = jnp.einsum(
        "kgqj,qkgd->jkd", shifts, query_grid, preferred_element_type=jnp.float32
    ).reshape(key_window.shape[0], -1)
    value_cot = jnp.einsum(
        "kgqj,qkgd->jkd",
        weights.astype(jnp.bfloat16),
        grad_grid,
        preferred_element_type=jnp.float32,
    ).reshape(key_window.shape[0], -1)
    return (query_cot, key_cot, value_cot)


def per_device(hidden, query_weight, key_weight, value_weight, query_gain, key_gain, out_grad):
    token_count = out_grad.shape[0]
    group_size = HEADS // KV_HEADS
    block_rows = min(token_count, 512)
    block_count = token_count // block_rows
    window_rows = block_rows + WINDOW
    reach_blocks = (WINDOW - 2) // token_count + 1
    position_base = lax.axis_index("ctx") * token_count
    gathered = gather_all(hidden, "heads")
    query_width = query_weight.shape[1]
    key_width = key_weight.shape[1]
    weight_cat = jnp.concatenate([query_weight, key_weight, value_weight], axis=1)
    projected = jnp.dot(gathered, weight_cat, preferred_element_type=jnp.float32)
    query_proj = projected[:, :query_width]
    key_proj = projected[:, query_width : query_width + key_width]
    value_proj = projected[:, query_width + key_width :]
    positions = position_base + jnp.arange(token_count, dtype=jnp.int32)
    cosine, sine_table = rope_tables(positions, HEAD_DIM)
    query_full, query_back = jax.vjp(
        lambda projected: prepare(projected, cosine, sine_table, query_gain, SCALAR ** (-0.5)),
        query_proj,
    )
    key_full, key_back = jax.vjp(
        lambda projected: prepare(projected, cosine, sine_table, key_gain, 1.0), key_proj
    )
    query_cast = query_full.astype(jnp.bfloat16)
    key_value = jnp.stack([key_full.astype(jnp.bfloat16), value_proj.astype(jnp.bfloat16)])
    received = [passed_along(key_value, "ctx", distance) for distance in range(1, reach_blocks + 1)]
    window_pair = jnp.concatenate(received[::-1] + [key_value], axis=1)
    key_span = window_pair[0]
    value_span = window_pair[1]

    def window_of(block_index):
        block_start = block_index * block_rows
        query_pos = position_base + block_start + jnp.arange(block_rows, dtype=jnp.int32)
        key_pos = position_base - WINDOW + block_start + jnp.arange(window_rows, dtype=jnp.int32)
        return (query_cast, key_span, value_span, band_mask(query_pos, key_pos))

    def forward_block(block_index):
        query_block, key_window, value_window, allowed = window_of(block_index)
        return attend_forward(query_block, key_window, value_window, allowed, group_size)

    outputs, log_totals = lax.map(forward_block, jnp.arange(block_count, dtype=jnp.int32))
    attention = outputs.reshape(token_count, -1).astype(jnp.bfloat16)

    def backward_block(block_index, carry):
        query_acc, pair_acc = carry
        query_block, key_window, value_window, allowed = window_of(block_index)
        block_start = block_index * block_rows
        query_cot, key_cot, value_cot = attend_backward(
            query_block,
            key_window,
            value_window,
            allowed,
            log_totals[block_index],
            out_grad,
            attention,
            group_size,
        )
        query_acc = query_cot
        region = pair_acc + jnp.stack([key_cot, value_cot])
        pair_acc = region
        return (query_acc, pair_acc)

    query_zero = jnp.zeros((token_count, query_weight.shape[1]), jnp.float32)
    pair_zero = jnp.zeros((2, (reach_blocks + 1) * token_count, key_weight.shape[1]), jnp.float32)
    query_acc, pair_acc = lax.fori_loop(0, block_count, backward_block, (query_zero, pair_zero))
    grad_query = query_back(query_acc)[0].astype(jnp.bfloat16)
    grad_scale = float(lax.axis_size("ctx") * token_count) ** (-0.5)
    contract = (((0,), (0,)), ((), ()))
    own_pair = pair_acc[:, reach_blocks * token_count :]
    for distance in range(1, reach_blocks + 1):
        lower_row = (reach_blocks - distance) * token_count
        own_pair = own_pair + passed_along(
            pair_acc[:, lower_row : lower_row + token_count].astype(jnp.bfloat16), "ctx", -distance
        ).astype(jnp.float32)
    grad_key = key_back(own_pair[0])[0].astype(jnp.bfloat16)
    grad_value = own_pair[1].astype(jnp.bfloat16)
    grad_cat = jnp.concatenate([grad_query, grad_key, grad_value], axis=1)
    back_contract = (((1,), (1,)), ((), ()))
    input_partial = lax.dot_general(
        grad_cat, weight_cat, back_contract, preferred_element_type=jnp.float32
    ).astype(jnp.bfloat16)
    input_partial, hidden_late = lax.optimization_barrier((input_partial, gathered))
    input_grad = exchange_sum(input_partial, "heads").astype(jnp.bfloat16)
    summed = ctx_scatter_sum(
        (
            lax.dot_general(hidden_late, grad_cat, contract, preferred_element_type=jnp.float32)
            * grad_scale
        ).astype(jnp.bfloat16),
        "ctx",
        (lax.axis_size("ctx") // 4, 2, 2),
    )
    query_weight_grad = summed[:, :query_width]
    key_weight_grad = summed[:, query_width : query_width + key_width]
    value_weight_grad = summed[:, query_width + key_width :]
    return (attention, input_grad, query_weight_grad, key_weight_grad, value_weight_grad)


def solution(mesh):
    return jax.shard_map(
        per_device,
        mesh=mesh,
        in_specs=(
            P(("ctx", "heads"), None),
            P(None, "heads"),
            P(None, "heads"),
            P(None, "heads"),
            P(),
            P(),
            P("ctx", "heads"),
        ),
        out_specs=(
            P("ctx", "heads"),
            P(("ctx", "heads"), None),
            P("ctx", "heads"),
            P("ctx", "heads"),
            P("ctx", "heads"),
        ),
        check_vma=False,
    )
```

```python
import math

import jax
import jax.numpy as jnp
from jax import lax
from jax.sharding import PartitionSpec as P

HEAD_DIM = 128
WINDOW = 1024
SCALAR = 168
HEADS = 16
KV_HEADS = 8


def passed_along(block, axis, distance):
    devices = range(lax.axis_size(axis))
    route = [(i - distance, i) for i in devices if i - distance in devices]
    return lax.ppermute(block, axis, route)


def torus_shifts(axis):
    size = lax.axis_size(axis)
    inner = size // 2 if size >= 4 else size
    outer = size // inner
    me = lax.axis_index(axis)

    def moved(index, dx, dy):
        return ((index // inner + dx) % outer) * inner + (index % inner + dy) % inner

    shifts = [(dx, dy) for dx in range(outer) for dy in range(inner)][1:]
    routes = [[(i, moved(i, dx, dy)) for i in range(size)] for dx, dy in shifts]
    targets = [moved(me, dx, dy) for dx, dy in shifts]
    slot_of = [
        ((me // inner - j // inner) % outer) * inner + (me % inner - j % inner) % inner
        for j in range(size)
    ]
    return (size, me, routes, targets, slot_of)


def gather_over(block, axis):
    size, me, routes, targets, slot_of = torus_shifts(axis)
    slots = jnp.stack([block] + [lax.ppermute(block, axis, route) for route in routes])
    order = jnp.stack([jnp.asarray(s, jnp.int32) for s in slot_of])
    return jnp.take(slots, order, axis=0).reshape((size * block.shape[0],) + block.shape[1:])


def scatter_sum_over(full, axis):
    size, me, routes, targets, slot_of = torus_shifts(axis)
    pieces = full.reshape((size, full.shape[0] // size) + full.shape[1:])
    total = lax.dynamic_index_in_dim(pieces, me, 0, keepdims=False).astype(jnp.float32)
    for route, target in zip(routes, targets):
        piece = lax.dynamic_index_in_dim(pieces, target, 0, keepdims=False)
        total = total + lax.ppermute(piece, axis, route).astype(jnp.float32)
    return total


def ring_scatter_sum(blocks, axis, count, stride):
    size = lax.axis_size(axis)
    me = lax.axis_index(axis)
    digit = (me // stride) % count
    half = blocks.shape[-1] // 2

    def route(step):
        return [
            (i, i - ((i // stride) % count) * stride + (((i // stride) % count + step) % count) * stride)
            for i in range(size)
        ]

    def chunk(k, step, lo):
        block = lax.dynamic_index_in_dim(blocks, (digit - step * (k + 1)) % count, 0, keepdims=False)
        return block[..., lo : lo + half]

    def advance(k, carry):
        up, down = carry
        up = lax.ppermute(up.astype(jnp.bfloat16), axis, route(1)).astype(jnp.float32)
        down = lax.ppermute(down.astype(jnp.bfloat16), axis, route(-1)).astype(jnp.float32)
        return (up + chunk(k + 1, 1, 0), down + chunk(k + 1, -1, half))

    up, down = lax.fori_loop(0, count - 1, advance, (chunk(0, 1, 0), chunk(0, -1, half)))
    return jnp.concatenate([up, down], axis=-1)


def pair_scatter_sum(blocks, axis, stride):
    size = lax.axis_size(axis)
    me = lax.axis_index(axis)
    digit = (me // stride) % 2
    route = [(i, i + stride if (i // stride) % 2 == 0 else i - stride) for i in range(size)]
    own = lax.dynamic_index_in_dim(blocks, digit, 0, keepdims=False).astype(jnp.float32)
    other = lax.dynamic_index_in_dim(blocks, 1 - digit, 0, keepdims=False)
    return own + lax.ppermute(other.astype(jnp.bfloat16), axis, route).astype(jnp.float32)


def ctx_scatter_sum(full, axis, levels):
    outer, middle, inner = levels
    width = full.shape[1]
    grid = full.reshape(outer, middle, inner, -1, width)
    grid = jnp.moveaxis(grid, 2, 0)
    grid = pair_scatter_sum(grid, axis, 1)
    grid = ring_scatter_sum(grid, axis, outer, middle * inner)
    return pair_scatter_sum(grid, axis, inner)


def gather_all(block, axis):
    size = lax.axis_size(axis)
    copies = jnp.broadcast_to(block[None], (size,) + block.shape)
    received = lax.all_to_all(copies, axis, 0, 0)
    return received.reshape((size * block.shape[0],) + block.shape[1:])


def exchange_sum(full, axis):
    size = lax.axis_size(axis)
    pieces = full.reshape((size, full.shape[0] // size) + full.shape[1:])
    received = lax.all_to_all(pieces, axis, 0, 0)
    return jnp.sum(received.astype(jnp.float32), axis=0)


def rope_tables(positions, head_size):
    half_size = head_size // 2
    indices = jnp.arange(half_size, dtype=jnp.float32)
    inverse = jnp.exp(indices * (-2.0 * math.log(10000.0) / head_size))
    angles = positions.astype(jnp.float32)[:, None] * inverse[None, :]
    return (jnp.cos(angles), jnp.sin(angles))


def prepare(projected, cosine, sine_table, channel_gain, factor):
    row_count = projected.shape[0]
    head_size = channel_gain.shape[0]
    pieces = projected.reshape(row_count, -1, head_size)
    normed = (
        pieces * lax.rsqrt(jnp.mean(pieces * pieces, axis=-1, keepdims=True) + 1e-06) * channel_gain
    )
    half_size = head_size // 2
    leading = normed[..., :half_size]
    trailing = normed[..., half_size:]
    cos_rows = cosine[:, None, :]
    sin_rows = sine_table[:, None, :]
    turned = jnp.concatenate(
        [leading * cos_rows - trailing * sin_rows, trailing * cos_rows + leading * sin_rows],
        axis=-1,
    )
    return (turned * factor).reshape(row_count, -1)


def band_mask(query_pos, key_pos):
    separation = query_pos[:, None] - key_pos[None, :]
    return (separation >= 0) & (separation < WINDOW) & (key_pos[None, :] >= 0)


def head_grids(query_block, key_window, value_window, group_size):
    query_grid = query_block.reshape(query_block.shape[0], -1, group_size, HEAD_DIM)
    key_grid = key_window.reshape(key_window.shape[0], -1, HEAD_DIM)
    value_grid = value_window.reshape(value_window.shape[0], -1, HEAD_DIM)
    return (query_grid, key_grid, value_grid)


def attend_forward(query_block, key_window, value_window, allowed, group_size):
    query_grid, key_grid, value_grid = head_grids(query_block, key_window, value_window, group_size)
    scores = jnp.einsum("qkgd,jkd->kgqj", query_grid, key_grid, preferred_element_type=jnp.float32)
    masked = jnp.where(allowed, scores, -1e30)
    highest = jnp.max(masked, axis=-1, keepdims=True)
    total = jnp.sum(jnp.exp(masked - highest), axis=-1, keepdims=True)
    log_total = highest + jnp.log(total)
    weights = jnp.where(allowed, jnp.exp(masked - log_total), 0.0)
    output = jnp.einsum(
        "kgqj,jkd->qkgd",
        weights.astype(jnp.bfloat16),
        value_grid,
        preferred_element_type=jnp.float32,
    )
    return (output.reshape(query_block.shape[0], -1), log_total[..., 0])


def attend_backward(
    query_block,
    key_window,
    value_window,
    allowed,
    log_total,
    out_block,
    attention_block,
    group_size,
):
    query_grid, key_grid, value_grid = head_grids(query_block, key_window, value_window, group_size)
    row_count = query_block.shape[0]
    grad_grid = out_block.reshape(row_count, -1, group_size, HEAD_DIM)
    attention_grid = attention_block.reshape(row_count, -1, group_size, HEAD_DIM)
    scores = jnp.einsum("qkgd,jkd->kgqj", query_grid, key_grid, preferred_element_type=jnp.float32)
    masked = jnp.where(allowed, scores, -1e30)
    weights = jnp.where(allowed, jnp.exp(masked - log_total[..., None]), 0.0)
    delta = jnp.einsum(
        "qkgd,qkgd->kgq", grad_grid, attention_grid, preferred_element_type=jnp.float32
    )
    products = jnp.einsum(
        "qkgd,jkd->kgqj", grad_grid, value_grid, preferred_element_type=jnp.float32
    )
    shifts = (weights * (products - delta[..., None])).astype(jnp.bfloat16)
    query_cot = jnp.einsum(
        "kgqj,jkd->qkgd", shifts, key_grid, preferred_element_type=jnp.float32
    ).reshape(row_count, -1)
    key_cot = jnp.einsum(
        "kgqj,qkgd->jkd", shifts, query_grid, preferred_element_type=jnp.float32
    ).reshape(key_window.shape[0], -1)
    value_cot = jnp.einsum(
        "kgqj,qkgd->jkd",
        weights.astype(jnp.bfloat16),
        grad_grid,
        preferred_element_type=jnp.float32,
    ).reshape(key_window.shape[0], -1)
    return (query_cot, key_cot, value_cot)


def per_device(hidden, query_weight, key_weight, value_weight, query_gain, key_gain, out_grad):
    token_count = out_grad.shape[0]
    group_size = HEADS // KV_HEADS
    block_rows = min(token_count, 512)
    block_count = token_count // block_rows
    window_rows = block_rows + WINDOW
    reach_blocks = (WINDOW - 2) // token_count + 1
    position_base = lax.axis_index("ctx") * token_count
    gathered = gather_all(hidden, "heads")
    query_width = query_weight.shape[1]
    key_width = key_weight.shape[1]
    weight_cat = jnp.concatenate([query_weight, key_weight, value_weight], axis=1)
    projected = jnp.dot(gathered, weight_cat, preferred_element_type=jnp.float32)
    query_proj = projected[:, :query_width]
    key_proj = projected[:, query_width : query_width + key_width]
    value_proj = projected[:, query_width + key_width :]
    positions = position_base + jnp.arange(token_count, dtype=jnp.int32)
    cosine, sine_table = rope_tables(positions, HEAD_DIM)
    query_full, query_back = jax.vjp(
        lambda projected: prepare(projected, cosine, sine_table, query_gain, SCALAR ** (-0.5)),
        query_proj,
    )
    key_full, key_back = jax.vjp(
        lambda projected: prepare(projected, cosine, sine_table, key_gain, 1.0), key_proj
    )
    query_cast = query_full.astype(jnp.bfloat16)
    key_value = jnp.stack([key_full.astype(jnp.bfloat16), value_proj.astype(jnp.bfloat16)])
    received = [passed_along(key_value, "ctx", distance) for distance in range(1, reach_blocks + 1)]
    window_pair = jnp.concatenate(received[::-1] + [key_value], axis=1)
    key_span = window_pair[0]
    value_span = window_pair[1]

    def window_of(block_index):
        block_start = block_index * block_rows
        query_pos = position_base + block_start + jnp.arange(block_rows, dtype=jnp.int32)
        key_pos = position_base - WINDOW + block_start + jnp.arange(window_rows, dtype=jnp.int32)
        return (query_cast, key_span, value_span, band_mask(query_pos, key_pos))

    def forward_block(block_index):
        query_block, key_window, value_window, allowed = window_of(block_index)
        return attend_forward(query_block, key_window, value_window, allowed, group_size)

    outputs, log_totals = lax.map(forward_block, jnp.arange(block_count, dtype=jnp.int32))
    attention = outputs.reshape(token_count, -1).astype(jnp.bfloat16)

    def backward_block(block_index, carry):
        query_acc, pair_acc = carry
        query_block, key_window, value_window, allowed = window_of(block_index)
        block_start = block_index * block_rows
        query_cot, key_cot, value_cot = attend_backward(
            query_block,
            key_window,
            value_window,
            allowed,
            log_totals[block_index],
            out_grad,
            attention,
            group_size,
        )
        query_acc = query_cot
        region = pair_acc + jnp.stack([key_cot, value_cot])
        pair_acc = region
        return (query_acc, pair_acc)

    query_zero = jnp.zeros((token_count, query_weight.shape[1]), jnp.float32)
    pair_zero = jnp.zeros((2, (reach_blocks + 1) * token_count, key_weight.shape[1]), jnp.float32)
    query_acc, pair_acc = lax.fori_loop(0, block_count, backward_block, (query_zero, pair_zero))
    grad_query = query_back(query_acc)[0].astype(jnp.bfloat16)
    grad_scale = float(lax.axis_size("ctx") * token_count) ** (-0.5)
    contract = (((0,), (0,)), ((), ()))
    query_product = (
        lax.dot_general(gathered, grad_query, contract, preferred_element_type=jnp.float32)
        * grad_scale
    ).astype(jnp.bfloat16)
    query_product, pair_acc = lax.optimization_barrier((query_product, pair_acc))
    query_weight_grad = lax.psum_scatter(
        query_product, "ctx", scatter_dimension=0, tiled=True
    ).astype(jnp.float32)
    own_pair = pair_acc[:, reach_blocks * token_count :]
    for distance in range(1, reach_blocks + 1):
        lower_row = (reach_blocks - distance) * token_count
        own_pair = own_pair + passed_along(
            pair_acc[:, lower_row : lower_row + token_count].astype(jnp.bfloat16), "ctx", -distance
        ).astype(jnp.float32)
    grad_key = key_back(own_pair[0])[0].astype(jnp.bfloat16)
    grad_value = own_pair[1].astype(jnp.bfloat16)
    grad_cat = jnp.concatenate([grad_query, grad_key, grad_value], axis=1)
    back_contract = (((1,), (1,)), ((), ()))
    input_partial = lax.dot_general(
        grad_cat, weight_cat, back_contract, preferred_element_type=jnp.float32
    ).astype(jnp.bfloat16)
    input_partial, hidden_late = lax.optimization_barrier((input_partial, gathered))
    input_grad = exchange_sum(input_partial, "heads").astype(jnp.bfloat16)
    pair_weight_grad = ctx_scatter_sum(
        (
            lax.dot_general(
                hidden_late,
                jnp.concatenate([grad_key, grad_value], axis=1),
                contract,
                preferred_element_type=jnp.float32,
            )
            * grad_scale
        ).astype(jnp.bfloat16),
        "ctx",
        (lax.axis_size("ctx") // 4, 2, 2),
    )
    key_weight_grad = pair_weight_grad[:, :key_width]
    value_weight_grad = pair_weight_grad[:, key_width:]
    return (attention, input_grad, query_weight_grad, key_weight_grad, value_weight_grad)


def solution(mesh):
    return jax.shard_map(
        per_device,
        mesh=mesh,
        in_specs=(
            P(("ctx", "heads"), None),
            P(None, "heads"),
            P(None, "heads"),
            P(None, "heads"),
            P(),
            P(),
            P("ctx", "heads"),
        ),
        out_specs=(
            P("ctx", "heads"),
            P(("ctx", "heads"), None),
            P("ctx", "heads"),
            P("ctx", "heads"),
            P("ctx", "heads"),
        ),
        check_vma=False,
    )
```

```python
import math

import jax
import jax.numpy as jnp
from jax import lax
from jax.sharding import PartitionSpec as P

HEAD_DIM = 128
WINDOW = 1024
SCALAR = 168
HEADS = 16
KV_HEADS = 8


def passed_along(block, axis, distance):
    devices = range(lax.axis_size(axis))
    route = [(i - distance, i) for i in devices if i - distance in devices]
    return lax.ppermute(block, axis, route)


def torus_shifts(axis):
    size = lax.axis_size(axis)
    inner = size // 2 if size >= 4 else size
    outer = size // inner
    me = lax.axis_index(axis)

    def moved(index, dx, dy):
        return ((index // inner + dx) % outer) * inner + (index % inner + dy) % inner

    shifts = [(dx, dy) for dx in range(outer) for dy in range(inner)][1:]
    routes = [[(i, moved(i, dx, dy)) for i in range(size)] for dx, dy in shifts]
    targets = [moved(me, dx, dy) for dx, dy in shifts]
    slot_of = [
        ((me // inner - j // inner) % outer) * inner + (me % inner - j % inner) % inner
        for j in range(size)
    ]
    return (size, me, routes, targets, slot_of)


def gather_over(block, axis):
    size, me, routes, targets, slot_of = torus_shifts(axis)
    slots = jnp.stack([block] + [lax.ppermute(block, axis, route) for route in routes])
    order = jnp.stack([jnp.asarray(s, jnp.int32) for s in slot_of])
    return jnp.take(slots, order, axis=0).reshape((size * block.shape[0],) + block.shape[1:])


def scatter_sum_over(full, axis):
    size, me, routes, targets, slot_of = torus_shifts(axis)
    pieces = full.reshape((size, full.shape[0] // size) + full.shape[1:])
    total = lax.dynamic_index_in_dim(pieces, me, 0, keepdims=False).astype(jnp.float32)
    for route, target in zip(routes, targets):
        piece = lax.dynamic_index_in_dim(pieces, target, 0, keepdims=False)
        total = total + lax.ppermute(piece, axis, route).astype(jnp.float32)
    return total


def ring_scatter_sum(blocks, axis, count, stride):
    size = lax.axis_size(axis)
    me = lax.axis_index(axis)
    digit = (me // stride) % count
    half = blocks.shape[-1] // 2

    def route(step):
        return [
            (i, i - ((i // stride) % count) * stride + (((i // stride) % count + step) % count) * stride)
            for i in range(size)
        ]

    def chunk(k, step, lo):
        block = lax.dynamic_index_in_dim(blocks, (digit - step * (k + 1)) % count, 0, keepdims=False)
        return block[..., lo : lo + half]

    def advance(k, carry):
        up, down = carry
        up = lax.ppermute(up.astype(jnp.bfloat16), axis, route(1)).astype(jnp.float32)
        down = lax.ppermute(down.astype(jnp.bfloat16), axis, route(-1)).astype(jnp.float32)
        return (up + chunk(k + 1, 1, 0), down + chunk(k + 1, -1, half))

    up, down = lax.fori_loop(0, count - 1, advance, (chunk(0, 1, 0), chunk(0, -1, half)))
    return jnp.concatenate([up, down], axis=-1)


def pair_scatter_sum(blocks, axis, stride):
    size = lax.axis_size(axis)
    me = lax.axis_index(axis)
    digit = (me // stride) % 2
    route = [(i, i + stride if (i // stride) % 2 == 0 else i - stride) for i in range(size)]
    own = lax.dynamic_index_in_dim(blocks, digit, 0, keepdims=False).astype(jnp.float32)
    other = lax.dynamic_index_in_dim(blocks, 1 - digit, 0, keepdims=False)
    return own + lax.ppermute(other.astype(jnp.bfloat16), axis, route).astype(jnp.float32)


def ctx_scatter_sum(full, axis, levels):
    outer, middle, inner = levels
    width = full.shape[1]
    grid = full.reshape(outer, middle, inner, -1, width)
    grid = jnp.moveaxis(grid, 2, 0)
    grid = pair_scatter_sum(grid, axis, 1)
    grid = ring_scatter_sum(grid, axis, outer, middle * inner)
    return pair_scatter_sum(grid, axis, inner)


def gather_all(block, axis):
    size = lax.axis_size(axis)
    copies = jnp.broadcast_to(block[None], (size,) + block.shape)
    received = lax.all_to_all(copies, axis, 0, 0)
    return received.reshape((size * block.shape[0],) + block.shape[1:])


def exchange_sum(full, axis):
    size = lax.axis_size(axis)
    pieces = full.reshape((size, full.shape[0] // size) + full.shape[1:])
    received = lax.all_to_all(pieces, axis, 0, 0)
    return jnp.sum(received.astype(jnp.float32), axis=0)


def rope_tables(positions, head_size):
    half_size = head_size // 2
    indices = jnp.arange(half_size, dtype=jnp.float32)
    inverse = jnp.exp(indices * (-2.0 * math.log(10000.0) / head_size))
    angles = positions.astype(jnp.float32)[:, None] * inverse[None, :]
    return (jnp.cos(angles), jnp.sin(angles))


def prepare(projected, cosine, sine_table, channel_gain, factor):
    row_count = projected.shape[0]
    head_size = channel_gain.shape[0]
    pieces = projected.reshape(row_count, -1, head_size)
    normed = (
        pieces * lax.rsqrt(jnp.mean(pieces * pieces, axis=-1, keepdims=True) + 1e-06) * channel_gain
    )
    half_size = head_size // 2
    leading = normed[..., :half_size]
    trailing = normed[..., half_size:]
    cos_rows = cosine[:, None, :]
    sin_rows = sine_table[:, None, :]
    turned = jnp.concatenate(
        [leading * cos_rows - trailing * sin_rows, trailing * cos_rows + leading * sin_rows],
        axis=-1,
    )
    return (turned * factor).reshape(row_count, -1)


def band_mask(query_pos, key_pos):
    separation = query_pos[:, None] - key_pos[None, :]
    return (separation >= 0) & (separation < WINDOW) & (key_pos[None, :] >= 0)


def head_grids(query_block, key_window, value_window, group_size):
    query_grid = query_block.reshape(query_block.shape[0], -1, group_size, HEAD_DIM)
    key_grid = key_window.reshape(key_window.shape[0], -1, HEAD_DIM)
    value_grid = value_window.reshape(value_window.shape[0], -1, HEAD_DIM)
    return (query_grid, key_grid, value_grid)


def attend_forward(query_block, key_window, value_window, allowed, group_size):
    query_grid, key_grid, value_grid = head_grids(query_block, key_window, value_window, group_size)
    scores = jnp.einsum("qkgd,jkd->kgqj", query_grid, key_grid, preferred_element_type=jnp.float32)
    masked = jnp.where(allowed, scores, -1e30)
    highest = jnp.max(masked, axis=-1, keepdims=True)
    total = jnp.sum(jnp.exp(masked - highest), axis=-1, keepdims=True)
    log_total = highest + jnp.log(total)
    weights = jnp.where(allowed, jnp.exp(masked - log_total), 0.0)
    output = jnp.einsum(
        "kgqj,jkd->qkgd",
        weights.astype(jnp.bfloat16),
        value_grid,
        preferred_element_type=jnp.float32,
    )
    return (output.reshape(query_block.shape[0], -1), log_total[..., 0])


def attend_backward(
    query_block,
    key_window,
    value_window,
    allowed,
    log_total,
    out_block,
    attention_block,
    group_size,
):
    query_grid, key_grid, value_grid = head_grids(query_block, key_window, value_window, group_size)
    row_count = query_block.shape[0]
    grad_grid = out_block.reshape(row_count, -1, group_size, HEAD_DIM)
    attention_grid = attention_block.reshape(row_count, -1, group_size, HEAD_DIM)
    scores = jnp.einsum("qkgd,jkd->kgqj", query_grid, key_grid, preferred_element_type=jnp.float32)
    masked = jnp.where(allowed, scores, -1e30)
    weights = jnp.where(allowed, jnp.exp(masked - log_total[..., None]), 0.0)
    delta = jnp.einsum(
        "qkgd,qkgd->kgq", grad_grid, attention_grid, preferred_element_type=jnp.float32
    )
    products = jnp.einsum(
        "qkgd,jkd->kgqj", grad_grid, value_grid, preferred_element_type=jnp.float32
    )
    shifts = (weights * (products - delta[..., None])).astype(jnp.bfloat16)
    query_cot = jnp.einsum(
        "kgqj,jkd->qkgd", shifts, key_grid, preferred_element_type=jnp.float32
    ).reshape(row_count, -1)
    key_cot = jnp.einsum(
        "kgqj,qkgd->jkd", shifts, query_grid, preferred_element_type=jnp.float32
    ).reshape(key_window.shape[0], -1)
    value_cot = jnp.einsum(
        "kgqj,qkgd->jkd",
        weights.astype(jnp.bfloat16),
        grad_grid,
        preferred_element_type=jnp.float32,
    ).reshape(key_window.shape[0], -1)
    return (query_cot, key_cot, value_cot)


def per_device(hidden, query_weight, key_weight, value_weight, query_gain, key_gain, out_grad):
    token_count = out_grad.shape[0]
    group_size = HEADS // KV_HEADS
    block_rows = min(token_count, 512)
    block_count = token_count // block_rows
    window_rows = block_rows + WINDOW
    reach_blocks = (WINDOW - 2) // token_count + 1
    position_base = lax.axis_index("ctx") * token_count
    gathered = gather_all(hidden, "heads")
    query_width = query_weight.shape[1]
    key_width = key_weight.shape[1]
    weight_cat = jnp.concatenate([query_weight, key_weight, value_weight], axis=1)
    projected = jnp.dot(gathered, weight_cat, preferred_element_type=jnp.float32)
    query_proj = projected[:, :query_width]
    key_proj = projected[:, query_width : query_width + key_width]
    value_proj = projected[:, query_width + key_width :]
    positions = position_base + jnp.arange(token_count, dtype=jnp.int32)
    cosine, sine_table = rope_tables(positions, HEAD_DIM)
    query_full, query_back = jax.vjp(
        lambda projected: prepare(projected, cosine, sine_table, query_gain, SCALAR ** (-0.5)),
        query_proj,
    )
    key_full, key_back = jax.vjp(
        lambda projected: prepare(projected, cosine, sine_table, key_gain, 1.0), key_proj
    )
    query_cast = query_full.astype(jnp.bfloat16)
    key_value = jnp.stack([key_full.astype(jnp.bfloat16), value_proj.astype(jnp.bfloat16)])
    received = [passed_along(key_value, "ctx", distance) for distance in range(1, reach_blocks + 1)]
    window_pair = jnp.concatenate(received[::-1] + [key_value], axis=1)
    key_span = window_pair[0]
    value_span = window_pair[1]

    def window_of(block_index):
        block_start = block_index * block_rows
        query_pos = position_base + block_start + jnp.arange(block_rows, dtype=jnp.int32)
        key_pos = position_base - WINDOW + block_start + jnp.arange(window_rows, dtype=jnp.int32)
        return (query_cast, key_span, value_span, band_mask(query_pos, key_pos))

    def forward_block(block_index):
        query_block, key_window, value_window, allowed = window_of(block_index)
        return attend_forward(query_block, key_window, value_window, allowed, group_size)

    outputs, log_totals = lax.map(forward_block, jnp.arange(block_count, dtype=jnp.int32))
    attention = outputs.reshape(token_count, -1).astype(jnp.bfloat16)

    def backward_block(block_index, carry):
        query_acc, pair_acc = carry
        query_block, key_window, value_window, allowed = window_of(block_index)
        block_start = block_index * block_rows
        query_cot, key_cot, value_cot = attend_backward(
            query_block,
            key_window,
            value_window,
            allowed,
            log_totals[block_index],
            out_grad,
            attention,
            group_size,
        )
        query_acc = query_cot
        region = pair_acc + jnp.stack([key_cot, value_cot])
        pair_acc = region
        return (query_acc, pair_acc)

    query_zero = jnp.zeros((token_count, query_weight.shape[1]), jnp.float32)
    pair_zero = jnp.zeros((2, (reach_blocks + 1) * token_count, key_weight.shape[1]), jnp.float32)
    query_acc, pair_acc = lax.fori_loop(0, block_count, backward_block, (query_zero, pair_zero))
    grad_query = query_back(query_acc)[0].astype(jnp.bfloat16)
    grad_scale = float(lax.axis_size("ctx") * token_count) ** (-0.5)
    contract = (((0,), (0,)), ((), ()))
    query_product = (
        lax.dot_general(gathered, grad_query, contract, preferred_element_type=jnp.float32)
        * grad_scale
    ).astype(jnp.bfloat16)
    query_product, pair_acc = lax.optimization_barrier((query_product, pair_acc))
    query_weight_grad = exchange_sum(query_product, "ctx")
    own_pair = pair_acc[:, reach_blocks * token_count :]
    for distance in range(1, reach_blocks + 1):
        lower_row = (reach_blocks - distance) * token_count
        own_pair = own_pair + passed_along(
            pair_acc[:, lower_row : lower_row + token_count].astype(jnp.bfloat16), "ctx", -distance
        ).astype(jnp.float32)
    grad_key = key_back(own_pair[0])[0].astype(jnp.bfloat16)
    grad_value = own_pair[1].astype(jnp.bfloat16)
    grad_cat = jnp.concatenate([grad_query, grad_key, grad_value], axis=1)
    back_contract = (((1,), (1,)), ((), ()))
    input_partial = lax.dot_general(
        grad_cat, weight_cat, back_contract, preferred_element_type=jnp.float32
    ).astype(jnp.bfloat16)
    input_partial, hidden_late, query_weight_grad = lax.optimization_barrier(
        (input_partial, gathered, query_weight_grad)
    )
    input_grad = exchange_sum(input_partial, "heads").astype(jnp.bfloat16)
    pair_weight_grad = ctx_scatter_sum(
        (
            lax.dot_general(
                hidden_late,
                jnp.concatenate([grad_key, grad_value], axis=1),
                contract,
                preferred_element_type=jnp.float32,
            )
            * grad_scale
        ).astype(jnp.bfloat16),
        "ctx",
        (lax.axis_size("ctx") // 4, 2, 2),
    )
    key_weight_grad = pair_weight_grad[:, :key_width]
    value_weight_grad = pair_weight_grad[:, key_width:]
    return (attention, input_grad, query_weight_grad, key_weight_grad, value_weight_grad)


def solution(mesh):
    return jax.shard_map(
        per_device,
        mesh=mesh,
        in_specs=(
            P(("ctx", "heads"), None),
            P(None, "heads"),
            P(None, "heads"),
            P(None, "heads"),
            P(),
            P(),
            P("ctx", "heads"),
        ),
        out_specs=(
            P("ctx", "heads"),
            P(("ctx", "heads"), None),
            P("ctx", "heads"),
            P("ctx", "heads"),
            P("ctx", "heads"),
        ),
        check_vma=False,
    )
```

```python
import math

import jax
import jax.numpy as jnp
from jax import lax
from jax.sharding import PartitionSpec as P

HEAD_DIM = 128
WINDOW = 1024
SCALAR = 168
HEADS = 16
KV_HEADS = 8


def passed_along(block, axis, distance):
    devices = range(lax.axis_size(axis))
    route = [(i - distance, i) for i in devices if i - distance in devices]
    return lax.ppermute(block, axis, route)


def torus_shifts(axis):
    size = lax.axis_size(axis)
    inner = size // 2 if size >= 4 else size
    outer = size // inner
    me = lax.axis_index(axis)

    def moved(index, dx, dy):
        return ((index // inner + dx) % outer) * inner + (index % inner + dy) % inner

    shifts = [(dx, dy) for dx in range(outer) for dy in range(inner)][1:]
    routes = [[(i, moved(i, dx, dy)) for i in range(size)] for dx, dy in shifts]
    targets = [moved(me, dx, dy) for dx, dy in shifts]
    slot_of = [
        ((me // inner - j // inner) % outer) * inner + (me % inner - j % inner) % inner
        for j in range(size)
    ]
    return (size, me, routes, targets, slot_of)


def gather_over(block, axis):
    size, me, routes, targets, slot_of = torus_shifts(axis)
    slots = jnp.stack([block] + [lax.ppermute(block, axis, route) for route in routes])
    order = jnp.stack([jnp.asarray(s, jnp.int32) for s in slot_of])
    return jnp.take(slots, order, axis=0).reshape((size * block.shape[0],) + block.shape[1:])


def scatter_sum_over(full, axis):
    size, me, routes, targets, slot_of = torus_shifts(axis)
    pieces = full.reshape((size, full.shape[0] // size) + full.shape[1:])
    total = lax.dynamic_index_in_dim(pieces, me, 0, keepdims=False).astype(jnp.float32)
    for route, target in zip(routes, targets):
        piece = lax.dynamic_index_in_dim(pieces, target, 0, keepdims=False)
        total = total + lax.ppermute(piece, axis, route).astype(jnp.float32)
    return total


def ring_scatter_sum(blocks, axis, count, stride):
    size = lax.axis_size(axis)
    me = lax.axis_index(axis)
    digit = (me // stride) % count
    half = blocks.shape[-1] // 2

    def route(step):
        return [
            (i, i - ((i // stride) % count) * stride + (((i // stride) % count + step) % count) * stride)
            for i in range(size)
        ]

    def chunk(k, step, lo):
        block = lax.dynamic_index_in_dim(blocks, (digit - step * (k + 1)) % count, 0, keepdims=False)
        return block[..., lo : lo + half]

    def advance(k, carry):
        up, down = carry
        up = lax.ppermute(up.astype(jnp.bfloat16), axis, route(1)).astype(jnp.float32)
        down = lax.ppermute(down.astype(jnp.bfloat16), axis, route(-1)).astype(jnp.float32)
        return (up + chunk(k + 1, 1, 0), down + chunk(k + 1, -1, half))

    up, down = lax.fori_loop(0, count - 1, advance, (chunk(0, 1, 0), chunk(0, -1, half)))
    return jnp.concatenate([up, down], axis=-1)


def pair_scatter_sum(blocks, axis, stride):
    size = lax.axis_size(axis)
    me = lax.axis_index(axis)
    digit = (me // stride) % 2
    route = [(i, i + stride if (i // stride) % 2 == 0 else i - stride) for i in range(size)]
    own = lax.dynamic_index_in_dim(blocks, digit, 0, keepdims=False).astype(jnp.float32)
    other = lax.dynamic_index_in_dim(blocks, 1 - digit, 0, keepdims=False)
    return own + lax.ppermute(other.astype(jnp.bfloat16), axis, route).astype(jnp.float32)


def ctx_scatter_sum(full, axis, levels):
    outer, middle, inner = levels
    width = full.shape[1]
    grid = full.reshape(outer, middle, inner, -1, width)
    grid = jnp.moveaxis(grid, 2, 0)
    grid = pair_scatter_sum(grid, axis, 1)
    grid = pair_scatter_sum(jnp.moveaxis(grid, 1, 0), axis, inner)
    return ring_scatter_sum(grid, axis, outer, middle * inner)


def gather_all(block, axis):
    size = lax.axis_size(axis)
    copies = jnp.broadcast_to(block[None], (size,) + block.shape)
    received = lax.all_to_all(copies, axis, 0, 0)
    return received.reshape((size * block.shape[0],) + block.shape[1:])


def exchange_sum(full, axis):
    size = lax.axis_size(axis)
    pieces = full.reshape((size, full.shape[0] // size) + full.shape[1:])
    received = lax.all_to_all(pieces, axis, 0, 0)
    return jnp.sum(received.astype(jnp.float32), axis=0)


def rope_tables(positions, head_size):
    half_size = head_size // 2
    indices = jnp.arange(half_size, dtype=jnp.float32)
    inverse = jnp.exp(indices * (-2.0 * math.log(10000.0) / head_size))
    angles = positions.astype(jnp.float32)[:, None] * inverse[None, :]
    return (jnp.cos(angles), jnp.sin(angles))


def prepare(projected, cosine, sine_table, channel_gain, factor):
    row_count = projected.shape[0]
    head_size = channel_gain.shape[0]
    pieces = projected.reshape(row_count, -1, head_size)
    normed = (
        pieces * lax.rsqrt(jnp.mean(pieces * pieces, axis=-1, keepdims=True) + 1e-06) * channel_gain
    )
    half_size = head_size // 2
    leading = normed[..., :half_size]
    trailing = normed[..., half_size:]
    cos_rows = cosine[:, None, :]
    sin_rows = sine_table[:, None, :]
    turned = jnp.concatenate(
        [leading * cos_rows - trailing * sin_rows, trailing * cos_rows + leading * sin_rows],
        axis=-1,
    )
    return (turned * factor).reshape(row_count, -1)


def band_mask(query_pos, key_pos):
    separation = query_pos[:, None] - key_pos[None, :]
    return (separation >= 0) & (separation < WINDOW) & (key_pos[None, :] >= 0)


def head_grids(query_block, key_window, value_window, group_size):
    query_grid = query_block.reshape(query_block.shape[0], -1, group_size, HEAD_DIM)
    key_grid = key_window.reshape(key_window.shape[0], -1, HEAD_DIM)
    value_grid = value_window.reshape(value_window.shape[0], -1, HEAD_DIM)
    return (query_grid, key_grid, value_grid)


def attend_forward(query_block, key_window, value_window, allowed, group_size):
    query_grid, key_grid, value_grid = head_grids(query_block, key_window, value_window, group_size)
    scores = jnp.einsum("qkgd,jkd->kgqj", query_grid, key_grid, preferred_element_type=jnp.float32)
    masked = jnp.where(allowed, scores, -1e30)
    highest = jnp.max(masked, axis=-1, keepdims=True)
    total = jnp.sum(jnp.exp(masked - highest), axis=-1, keepdims=True)
    log_total = highest + jnp.log(total)
    weights = jnp.where(allowed, jnp.exp(masked - log_total), 0.0)
    output = jnp.einsum(
        "kgqj,jkd->qkgd",
        weights.astype(jnp.bfloat16),
        value_grid,
        preferred_element_type=jnp.float32,
    )
    return (output.reshape(query_block.shape[0], -1), log_total[..., 0])


def attend_backward(
    query_block,
    key_window,
    value_window,
    allowed,
    log_total,
    out_block,
    attention_block,
    group_size,
):
    query_grid, key_grid, value_grid = head_grids(query_block, key_window, value_window, group_size)
    row_count = query_block.shape[0]
    grad_grid = out_block.reshape(row_count, -1, group_size, HEAD_DIM)
    attention_grid = attention_block.reshape(row_count, -1, group_size, HEAD_DIM)
    scores = jnp.einsum("qkgd,jkd->kgqj", query_grid, key_grid, preferred_element_type=jnp.float32)
    masked = jnp.where(allowed, scores, -1e30)
    weights = jnp.where(allowed, jnp.exp(masked - log_total[..., None]), 0.0)
    delta = jnp.einsum(
        "qkgd,qkgd->kgq", grad_grid, attention_grid, preferred_element_type=jnp.float32
    )
    products = jnp.einsum(
        "qkgd,jkd->kgqj", grad_grid, value_grid, preferred_element_type=jnp.float32
    )
    shifts = (weights * (products - delta[..., None])).astype(jnp.bfloat16)
    query_cot = jnp.einsum(
        "kgqj,jkd->qkgd", shifts, key_grid, preferred_element_type=jnp.float32
    ).reshape(row_count, -1)
    key_cot = jnp.einsum(
        "kgqj,qkgd->jkd", shifts, query_grid, preferred_element_type=jnp.float32
    ).reshape(key_window.shape[0], -1)
    value_cot = jnp.einsum(
        "kgqj,qkgd->jkd",
        weights.astype(jnp.bfloat16),
        grad_grid,
        preferred_element_type=jnp.float32,
    ).reshape(key_window.shape[0], -1)
    return (query_cot, key_cot, value_cot)


def per_device(hidden, query_weight, key_weight, value_weight, query_gain, key_gain, out_grad):
    token_count = out_grad.shape[0]
    group_size = HEADS // KV_HEADS
    block_rows = min(token_count, 512)
    block_count = token_count // block_rows
    window_rows = block_rows + WINDOW
    reach_blocks = (WINDOW - 2) // token_count + 1
    position_base = lax.axis_index("ctx") * token_count
    gathered = gather_all(hidden, "heads")
    query_width = query_weight.shape[1]
    key_width = key_weight.shape[1]
    weight_cat = jnp.concatenate([query_weight, key_weight, value_weight], axis=1)
    projected = jnp.dot(gathered, weight_cat, preferred_element_type=jnp.float32)
    query_proj = projected[:, :query_width]
    key_proj = projected[:, query_width : query_width + key_width]
    value_proj = projected[:, query_width + key_width :]
    positions = position_base + jnp.arange(token_count, dtype=jnp.int32)
    cosine, sine_table = rope_tables(positions, HEAD_DIM)
    query_full, query_back = jax.vjp(
        lambda projected: prepare(projected, cosine, sine_table, query_gain, SCALAR ** (-0.5)),
        query_proj,
    )
    key_full, key_back = jax.vjp(
        lambda projected: prepare(projected, cosine, sine_table, key_gain, 1.0), key_proj
    )
    query_cast = query_full.astype(jnp.bfloat16)
    key_value = jnp.stack([key_full.astype(jnp.bfloat16), value_proj.astype(jnp.bfloat16)])
    received = [passed_along(key_value, "ctx", distance) for distance in range(1, reach_blocks + 1)]
    window_pair = jnp.concatenate(received[::-1] + [key_value], axis=1)
    key_span = window_pair[0]
    value_span = window_pair[1]

    def window_of(block_index):
        block_start = block_index * block_rows
        query_pos = position_base + block_start + jnp.arange(block_rows, dtype=jnp.int32)
        key_pos = position_base - WINDOW + block_start + jnp.arange(window_rows, dtype=jnp.int32)
        return (query_cast, key_span, value_span, band_mask(query_pos, key_pos))

    def forward_block(block_index):
        query_block, key_window, value_window, allowed = window_of(block_index)
        return attend_forward(query_block, key_window, value_window, allowed, group_size)

    outputs, log_totals = lax.map(forward_block, jnp.arange(block_count, dtype=jnp.int32))
    attention = outputs.reshape(token_count, -1).astype(jnp.bfloat16)

    def backward_block(block_index, carry):
        query_acc, pair_acc = carry
        query_block, key_window, value_window, allowed = window_of(block_index)
        block_start = block_index * block_rows
        query_cot, key_cot, value_cot = attend_backward(
            query_block,
            key_window,
            value_window,
            allowed,
            log_totals[block_index],
            out_grad,
            attention,
            group_size,
        )
        query_acc = query_cot
        region = pair_acc + jnp.stack([key_cot, value_cot])
        pair_acc = region
        return (query_acc, pair_acc)

    query_zero = jnp.zeros((token_count, query_weight.shape[1]), jnp.float32)
    pair_zero = jnp.zeros((2, (reach_blocks + 1) * token_count, key_weight.shape[1]), jnp.float32)
    query_acc, pair_acc = lax.fori_loop(0, block_count, backward_block, (query_zero, pair_zero))
    grad_query = query_back(query_acc)[0].astype(jnp.bfloat16)
    grad_scale = float(lax.axis_size("ctx") * token_count) ** (-0.5)
    contract = (((0,), (0,)), ((), ()))
    own_pair = pair_acc[:, reach_blocks * token_count :]
    for distance in range(1, reach_blocks + 1):
        lower_row = (reach_blocks - distance) * token_count
        own_pair = own_pair + passed_along(
            pair_acc[:, lower_row : lower_row + token_count].astype(jnp.bfloat16), "ctx", -distance
        ).astype(jnp.float32)
    grad_key = key_back(own_pair[0])[0].astype(jnp.bfloat16)
    grad_value = own_pair[1].astype(jnp.bfloat16)
    grad_cat = jnp.concatenate([grad_query, grad_key, grad_value], axis=1)
    back_contract = (((1,), (1,)), ((), ()))
    input_partial = lax.dot_general(
        grad_cat, weight_cat, back_contract, preferred_element_type=jnp.float32
    ).astype(jnp.bfloat16)
    input_partial, hidden_late = lax.optimization_barrier((input_partial, gathered))
    input_grad = exchange_sum(input_partial, "heads").astype(jnp.bfloat16)
    summed = ctx_scatter_sum(
        (
            lax.dot_general(hidden_late, grad_cat, contract, preferred_element_type=jnp.float32)
            * grad_scale
        ).astype(jnp.bfloat16),
        "ctx",
        (lax.axis_size("ctx") // 4, 2, 2),
    )
    query_weight_grad = summed[:, :query_width]
    key_weight_grad = summed[:, query_width : query_width + key_width]
    value_weight_grad = summed[:, query_width + key_width :]
    return (attention, input_grad, query_weight_grad, key_weight_grad, value_weight_grad)


def solution(mesh):
    return jax.shard_map(
        per_device,
        mesh=mesh,
        in_specs=(
            P(("ctx", "heads"), None),
            P(None, "heads"),
            P(None, "heads"),
            P(None, "heads"),
            P(),
            P(),
            P("ctx", "heads"),
        ),
        out_specs=(
            P("ctx", "heads"),
            P(("ctx", "heads"), None),
            P("ctx", "heads"),
            P("ctx", "heads"),
            P("ctx", "heads"),
        ),
        check_vma=False,
    )
```

```python
import math

import jax
import jax.numpy as jnp
from jax import lax
from jax.sharding import PartitionSpec as P

HEAD_DIM = 128
WINDOW = 1024
SCALAR = 168
HEADS = 16
KV_HEADS = 8


def passed_along(block, axis, distance):
    devices = range(lax.axis_size(axis))
    route = [(i - distance, i) for i in devices if i - distance in devices]
    return lax.ppermute(block, axis, route)


def torus_shifts(axis):
    size = lax.axis_size(axis)
    inner = size // 2 if size >= 4 else size
    outer = size // inner
    me = lax.axis_index(axis)

    def moved(index, dx, dy):
        return ((index // inner + dx) % outer) * inner + (index % inner + dy) % inner

    shifts = [(dx, dy) for dx in range(outer) for dy in range(inner)][1:]
    routes = [[(i, moved(i, dx, dy)) for i in range(size)] for dx, dy in shifts]
    targets = [moved(me, dx, dy) for dx, dy in shifts]
    slot_of = [
        ((me // inner - j // inner) % outer) * inner + (me % inner - j % inner) % inner
        for j in range(size)
    ]
    return (size, me, routes, targets, slot_of)


def gather_over(block, axis):
    size, me, routes, targets, slot_of = torus_shifts(axis)
    slots = jnp.stack([block] + [lax.ppermute(block, axis, route) for route in routes])
    order = jnp.stack([jnp.asarray(s, jnp.int32) for s in slot_of])
    return jnp.take(slots, order, axis=0).reshape((size * block.shape[0],) + block.shape[1:])


def scatter_sum_over(full, axis):
    size, me, routes, targets, slot_of = torus_shifts(axis)
    pieces = full.reshape((size, full.shape[0] // size) + full.shape[1:])
    total = lax.dynamic_index_in_dim(pieces, me, 0, keepdims=False).astype(jnp.float32)
    for route, target in zip(routes, targets):
        piece = lax.dynamic_index_in_dim(pieces, target, 0, keepdims=False)
        total = total + lax.ppermute(piece, axis, route).astype(jnp.float32)
    return total


def ring_scatter_sum(blocks, axis, count, stride):
    size = lax.axis_size(axis)
    me = lax.axis_index(axis)
    digit = (me // stride) % count
    half = blocks.shape[-1] // 2

    def route(step):
        return [
            (i, i - ((i // stride) % count) * stride + (((i // stride) % count + step) % count) * stride)
            for i in range(size)
        ]

    def chunk(k, step, lo):
        block = lax.dynamic_index_in_dim(blocks, (digit - step * (k + 1)) % count, 0, keepdims=False)
        return block[..., lo : lo + half]

    def advance(k, carry):
        up, down = carry
        up = lax.ppermute(up.astype(jnp.bfloat16), axis, route(1)).astype(jnp.float32)
        down = lax.ppermute(down.astype(jnp.bfloat16), axis, route(-1)).astype(jnp.float32)
        return (up + chunk(k + 1, 1, 0), down + chunk(k + 1, -1, half))

    up, down = lax.fori_loop(0, count - 1, advance, (chunk(0, 1, 0), chunk(0, -1, half)))
    return jnp.concatenate([up, down], axis=-1)


def pair_scatter_sum(blocks, axis, stride):
    size = lax.axis_size(axis)
    me = lax.axis_index(axis)
    digit = (me // stride) % 2
    route = [(i, i + stride if (i // stride) % 2 == 0 else i - stride) for i in range(size)]
    own = lax.dynamic_index_in_dim(blocks, digit, 0, keepdims=False).astype(jnp.float32)
    other = lax.dynamic_index_in_dim(blocks, 1 - digit, 0, keepdims=False)
    return own + lax.ppermute(other.astype(jnp.bfloat16), axis, route).astype(jnp.float32)


def ctx_scatter_sum(full, axis, levels):
    outer, middle, inner = levels
    width = full.shape[1]
    grid = full.reshape(outer, middle, inner, -1, width)
    grid = jnp.moveaxis(grid, 2, 0)
    grid = pair_scatter_sum(grid, axis, 1)
    return ring_scatter_sum(grid, axis, outer, middle * inner)


def gather_all(block, axis):
    size = lax.axis_size(axis)
    copies = jnp.broadcast_to(block[None], (size,) + block.shape)
    received = lax.all_to_all(copies, axis, 0, 0)
    return received.reshape((size * block.shape[0],) + block.shape[1:])


def exchange_sum(full, axis):
    size = lax.axis_size(axis)
    pieces = full.reshape((size, full.shape[0] // size) + full.shape[1:])
    received = lax.all_to_all(pieces, axis, 0, 0)
    return jnp.sum(received.astype(jnp.float32), axis=0)


def rope_tables(positions, head_size):
    half_size = head_size // 2
    indices = jnp.arange(half_size, dtype=jnp.float32)
    inverse = jnp.exp(indices * (-2.0 * math.log(10000.0) / head_size))
    angles = positions.astype(jnp.float32)[:, None] * inverse[None, :]
    return (jnp.cos(angles), jnp.sin(angles))


def prepare(projected, cosine, sine_table, channel_gain, factor):
    row_count = projected.shape[0]
    head_size = channel_gain.shape[0]
    pieces = projected.reshape(row_count, -1, head_size)
    normed = (
        pieces * lax.rsqrt(jnp.mean(pieces * pieces, axis=-1, keepdims=True) + 1e-06) * channel_gain
    )
    half_size = head_size // 2
    leading = normed[..., :half_size]
    trailing = normed[..., half_size:]
    cos_rows = cosine[:, None, :]
    sin_rows = sine_table[:, None, :]
    turned = jnp.concatenate(
        [leading * cos_rows - trailing * sin_rows, trailing * cos_rows + leading * sin_rows],
        axis=-1,
    )
    return (turned * factor).reshape(row_count, -1)


def band_mask(query_pos, key_pos):
    separation = query_pos[:, None] - key_pos[None, :]
    return (separation >= 0) & (separation < WINDOW) & (key_pos[None, :] >= 0)


def head_grids(query_block, key_window, value_window, group_size):
    query_grid = query_block.reshape(query_block.shape[0], -1, group_size, HEAD_DIM)
    key_grid = key_window.reshape(key_window.shape[0], -1, HEAD_DIM)
    value_grid = value_window.reshape(value_window.shape[0], -1, HEAD_DIM)
    return (query_grid, key_grid, value_grid)


def attend_forward(query_block, key_window, value_window, allowed, group_size):
    query_grid, key_grid, value_grid = head_grids(query_block, key_window, value_window, group_size)
    scores = jnp.einsum("qkgd,jkd->kgqj", query_grid, key_grid, preferred_element_type=jnp.float32)
    masked = jnp.where(allowed, scores, -1e30)
    highest = jnp.max(masked, axis=-1, keepdims=True)
    total = jnp.sum(jnp.exp(masked - highest), axis=-1, keepdims=True)
    log_total = highest + jnp.log(total)
    weights = jnp.where(allowed, jnp.exp(masked - log_total), 0.0)
    output = jnp.einsum(
        "kgqj,jkd->qkgd",
        weights.astype(jnp.bfloat16),
        value_grid,
        preferred_element_type=jnp.float32,
    )
    return (output.reshape(query_block.shape[0], -1), log_total[..., 0])


def attend_backward(
    query_block,
    key_window,
    value_window,
    allowed,
    log_total,
    out_block,
    attention_block,
    group_size,
):
    query_grid, key_grid, value_grid = head_grids(query_block, key_window, value_window, group_size)
    row_count = query_block.shape[0]
    grad_grid = out_block.reshape(row_count, -1, group_size, HEAD_DIM)
    attention_grid = attention_block.reshape(row_count, -1, group_size, HEAD_DIM)
    scores = jnp.einsum("qkgd,jkd->kgqj", query_grid, key_grid, preferred_element_type=jnp.float32)
    masked = jnp.where(allowed, scores, -1e30)
    weights = jnp.where(allowed, jnp.exp(masked - log_total[..., None]), 0.0)
    delta = jnp.einsum(
        "qkgd,qkgd->kgq", grad_grid, attention_grid, preferred_element_type=jnp.float32
    )
    products = jnp.einsum(
        "qkgd,jkd->kgqj", grad_grid, value_grid, preferred_element_type=jnp.float32
    )
    shifts = (weights * (products - delta[..., None])).astype(jnp.bfloat16)
    query_cot = jnp.einsum(
        "kgqj,jkd->qkgd", shifts, key_grid, preferred_element_type=jnp.float32
    ).reshape(row_count, -1)
    key_cot = jnp.einsum(
        "kgqj,qkgd->jkd", shifts, query_grid, preferred_element_type=jnp.float32
    ).reshape(key_window.shape[0], -1)
    value_cot = jnp.einsum(
        "kgqj,qkgd->jkd",
        weights.astype(jnp.bfloat16),
        grad_grid,
        preferred_element_type=jnp.float32,
    ).reshape(key_window.shape[0], -1)
    return (query_cot, key_cot, value_cot)


def per_device(hidden, query_weight, key_weight, value_weight, query_gain, key_gain, out_grad):
    token_count = out_grad.shape[0]
    group_size = HEADS // KV_HEADS
    block_rows = min(token_count, 512)
    block_count = token_count // block_rows
    window_rows = block_rows + WINDOW
    reach_blocks = (WINDOW - 2) // token_count + 1
    position_base = lax.axis_index("ctx") * token_count
    gathered = gather_all(hidden, "heads")
    query_width = query_weight.shape[1]
    key_width = key_weight.shape[1]
    weight_cat = jnp.concatenate([query_weight, key_weight, value_weight], axis=1)
    projected = jnp.dot(gathered, weight_cat, preferred_element_type=jnp.float32)
    query_proj = projected[:, :query_width]
    key_proj = projected[:, query_width : query_width + key_width]
    value_proj = projected[:, query_width + key_width :]
    positions = position_base + jnp.arange(token_count, dtype=jnp.int32)
    cosine, sine_table = rope_tables(positions, HEAD_DIM)
    query_full, query_back = jax.vjp(
        lambda projected: prepare(projected, cosine, sine_table, query_gain, SCALAR ** (-0.5)),
        query_proj,
    )
    key_full, key_back = jax.vjp(
        lambda projected: prepare(projected, cosine, sine_table, key_gain, 1.0), key_proj
    )
    query_cast = query_full.astype(jnp.bfloat16)
    key_value = jnp.stack([key_full.astype(jnp.bfloat16), value_proj.astype(jnp.bfloat16)])
    received = [passed_along(key_value, "ctx", distance) for distance in range(1, reach_blocks + 1)]
    window_pair = jnp.concatenate(received[::-1] + [key_value], axis=1)
    key_span = window_pair[0]
    value_span = window_pair[1]

    def window_of(block_index):
        block_start = block_index * block_rows
        query_pos = position_base + block_start + jnp.arange(block_rows, dtype=jnp.int32)
        key_pos = position_base - WINDOW + block_start + jnp.arange(window_rows, dtype=jnp.int32)
        return (query_cast, key_span, value_span, band_mask(query_pos, key_pos))

    def forward_block(block_index):
        query_block, key_window, value_window, allowed = window_of(block_index)
        return attend_forward(query_block, key_window, value_window, allowed, group_size)

    outputs, log_totals = lax.map(forward_block, jnp.arange(block_count, dtype=jnp.int32))
    attention = outputs.reshape(token_count, -1).astype(jnp.bfloat16)

    def backward_block(block_index, carry):
        query_acc, pair_acc = carry
        query_block, key_window, value_window, allowed = window_of(block_index)
        block_start = block_index * block_rows
        query_cot, key_cot, value_cot = attend_backward(
            query_block,
            key_window,
            value_window,
            allowed,
            log_totals[block_index],
            out_grad,
            attention,
            group_size,
        )
        query_acc = query_cot
        region = pair_acc + jnp.stack([key_cot, value_cot])
        pair_acc = region
        return (query_acc, pair_acc)

    query_zero = jnp.zeros((token_count, query_weight.shape[1]), jnp.float32)
    pair_zero = jnp.zeros((2, (reach_blocks + 1) * token_count, key_weight.shape[1]), jnp.float32)
    query_acc, pair_acc = lax.fori_loop(0, block_count, backward_block, (query_zero, pair_zero))
    grad_query = query_back(query_acc)[0].astype(jnp.bfloat16)
    grad_scale = float(lax.axis_size("ctx") * token_count) ** (-0.5)
    contract = (((0,), (0,)), ((), ()))
    own_pair = pair_acc[:, reach_blocks * token_count :]
    for distance in range(1, reach_blocks + 1):
        lower_row = (reach_blocks - distance) * token_count
        own_pair = own_pair + passed_along(
            pair_acc[:, lower_row : lower_row + token_count].astype(jnp.bfloat16), "ctx", -distance
        ).astype(jnp.float32)
    grad_key = key_back(own_pair[0])[0].astype(jnp.bfloat16)
    grad_value = own_pair[1].astype(jnp.bfloat16)
    grad_cat = jnp.concatenate([grad_query, grad_key, grad_value], axis=1)
    back_contract = (((1,), (1,)), ((), ()))
    input_partial = lax.dot_general(
        grad_cat, weight_cat, back_contract, preferred_element_type=jnp.float32
    ).astype(jnp.bfloat16)
    input_partial, hidden_late = lax.optimization_barrier((input_partial, gathered))
    heads_size = lax.axis_size("heads")
    received = lax.all_to_all(
        input_partial.reshape((heads_size, -1) + input_partial.shape[1:]), "heads", 0, 0
    )
    summed = ctx_scatter_sum(
        (
            lax.dot_general(hidden_late, grad_cat, contract, preferred_element_type=jnp.float32)
            * grad_scale
        ).astype(jnp.bfloat16),
        "ctx",
        (lax.axis_size("ctx") // 4, 2, 2),
    )
    summed, received = lax.optimization_barrier((summed, received))
    summed = pair_scatter_sum(summed, "ctx", 2)
    input_grad = jnp.sum(received.astype(jnp.float32), axis=0).astype(jnp.bfloat16)
    query_weight_grad = summed[:, :query_width]
    key_weight_grad = summed[:, query_width : query_width + key_width]
    value_weight_grad = summed[:, query_width + key_width :]
    return (attention, input_grad, query_weight_grad, key_weight_grad, value_weight_grad)


def solution(mesh):
    return jax.shard_map(
        per_device,
        mesh=mesh,
        in_specs=(
            P(("ctx", "heads"), None),
            P(None, "heads"),
            P(None, "heads"),
            P(None, "heads"),
            P(),
            P(),
            P("ctx", "heads"),
        ),
        out_specs=(
            P("ctx", "heads"),
            P(("ctx", "heads"), None),
            P("ctx", "heads"),
            P("ctx", "heads"),
            P("ctx", "heads"),
        ),
        check_vma=False,
    )
```
